512 devices in a mesh: lat: 4 (over x_lo, core), lon: 128 (over y, z, x_hi).
Axes of the slice: x: 4 (x_hi: 2, x_lo: 2; x = x_hi * 2 + x_lo), y: 8, z: 8, core: 2. Of those that a mesh axis runs over, the one named last changes fastest.
Arguments:
- moisture: float32 [32, 128, 32768], P(None, 'lat', 'lon'), may hold values from 0.05 to 0.45
- conductance: float32 [128, 32768], P('lat', 'lon'), may hold values from 0.08 to 0.24
- inverse: float32 [128, 256, 1024], P('lat', 'lon'), may hold values from -1 to 1, as said below
- crop_mask: int32 [128, 32768], P('lat', 'lon'), may hold values 0 or 1
- adjoint_in: float32 [32, 128, 32768], P(None, 'lat', 'lon'), may hold values from -6 to 6
- foot_anchor: int32 [4, 128, 128, 2], P('lat', 'lon'), may hold values from -1 to 6384, as said below
- antenna_gain: float32 [4, 128, 128, 2, 512], P('lat', 'lon'), may hold values from -0.25 to 0.25
- obs_value: float32 [4, 128, 128, 2], P('lat', 'lon'), may hold values from -6 to 6
- obs_weight: float32 [4, 128, 128, 2], P('lat', 'lon'), may hold values from 0.5 to 5
Outputs:
- gradient: float32 [32, 128, 32768], P(None, 'lat', 'lon')
- residual: float32 [4, 128, 128, 2], P('lat', 'lon')
The draws below stay inside these ranges and needn't reach their ends.
Inputs may be any that keep to these rules, and one draw needn't show every extreme that they name: `foot_anchor`: every live window lies inside its tile; some owner column receives all 2 slots live from every tile; some tiles fill all their slots. `inverse`: each matrix has a positive diagonal of 0.6 to 1.
All inputs are finite; a program needn't handle non-finite values. No bound on the sum of `crop_mask` on one device may be relied on, other than what follows from the above.
Results may differ from the reference program's by a relative error of at most 0.00005.
Values sent between devices are 32-bit elements; how exact they have to be, the bound alone decides.
No kernel may reach another device: no remote copies, remote signals or barrier semaphores. Data moves between devices by JAX's collectives and lax.ppermute only.
A program may use at most 64 MiB of HBM per device.

```python
import math
import jax
import jax.numpy as jnp
from jax import lax

L = 32
LG = 8
LTOP = 4
FH = 8
FW = 16
CAP = 2
CLAT = 32
CLON = 256
NLAT = 128
NLON = 32768
NBLK = 256
K = 512
N_LAT = 4
N_LON = 128


def draw_inverse(key, part):
    first, second = jax.random.split(key)
    shape = (NLAT, NBLK, L * L)
    flat = lax.broadcasted_iota(jnp.int32, shape, 2)
    on_diag = flat // L == flat % L
    offdiag = jax.random.normal(first, shape, jnp.float32) * (1.0 / math.sqrt(L))
    offdiag = jnp.clip(offdiag, -1.0, 1.0)
    diagonal = jax.random.uniform(second, shape, jnp.float32, 0.6, 1.0)
    return jnp.where(on_diag, diagonal, offdiag)


def draw_foot_anchor(key, part):
    keys = jax.random.split(key, 5)
    shape = (N_LAT, N_LON, N_LON, CAP)
    rows_pick = jax.random.randint(keys[0], shape, 0, CLAT - FH + 1)
    cols_pick = jax.random.randint(keys[1], shape, 0, CLON - FW + 1)
    anchor = rows_pick * CLON + cols_pick
    dense_tile = jax.random.randint(keys[2], (N_LAT, N_LON, 1, 1), 0, 4) == 0
    full_owner = jax.random.randint(keys[3], (), 0, N_LON)
    coin = jax.random.randint(keys[4], shape, 0, 10) < 3
    owner = lax.broadcasted_iota(jnp.int32, shape, 2)
    keep = dense_tile | coin | (owner == full_owner)
    first_slot = (lax.broadcasted_iota(jnp.int32, shape, 0) == 0) & (lax.broadcasted_iota(jnp.int32, shape, 1) == 0) & (lax.broadcasted_iota(jnp.int32, shape, 3) == 0) & (owner == full_owner)
    anchor = jnp.where(first_slot, (CLAT - FH) * CLON + CLON - FW, anchor)
    return jnp.where(keep, anchor, -1).astype(jnp.int32)


def with_ends(array, own_key, least, high):
    place = [jax.random.randint(jax.random.fold_in(own_key, axis), (), 0, length) for axis, length in enumerate(array.shape)]
    widest = array.shape.index(max(array.shape))
    beside = place[:widest] + [(place[widest] + 1) % array.shape[widest]] + place[widest + 1:]
    return array.at[tuple(place)].set(least).at[tuple(beside)].set(high)


def block_levels(rng, extent, cuts, smallest, high):
    loudness = 1.0
    for dim, parts in cuts:
        heights = jax.random.uniform(jax.random.fold_in(jax.random.fold_in(rng, 6), dim), (parts,), jnp.float32, smallest / len(cuts), high / len(cuts))
        loudness = loudness * jnp.repeat(jnp.exp(heights), extent[dim] // parts).reshape((-1,) + (1,) * (len(extent) - 1 - dim))
    return loudness


def normal_values(rng, shape, width, most, pieces=(), kind=jnp.bfloat16):
    array = width * jax.random.normal(rng, shape, jnp.float32)
    if pieces:
        array = array * block_levels(rng, shape, pieces, -0.22, 0.18)
    return jnp.clip(array, -most, most).astype(kind)


def setup_inputs(seed: int = 0) -> dict:
    arg_keys = jax.random.split(jax.random.key(seed), 10)
    moisture = jnp.clip(0.05 + 0.39999999 * jax.random.uniform(arg_keys[0], (L, NLAT, NLON), jnp.float32) ** block_levels(arg_keys[0], (L, NLAT, NLON), ((1, 4), (2, 128)), -0.2, 0.2), 0.05, 0.45)
    conductance = jnp.clip(0.08 + 0.16 * jax.random.uniform(arg_keys[1], (NLAT, NLON), jnp.float32) ** block_levels(arg_keys[1], (NLAT, NLON), ((0, 4), (1, 128)), -0.2, 0.2), 0.08, 0.24)
    inverse = draw_inverse(jax.random.fold_in(arg_keys[9], 71), 0)
    crop_mask = with_ends((jax.random.randint(arg_keys[3], (NLAT, NLON), 0, 2) < 1).astype(jnp.int32), jax.random.fold_in(arg_keys[3], 1), 0, 1)
    adjoint_in = normal_values(arg_keys[4], (L, NLAT, NLON), 1.0, 6.0, ((1, 4), (2, 128)), jnp.float32)
    foot_anchor = draw_foot_anchor(jax.random.fold_in(arg_keys[9], 71), 0)
    antenna_gain = normal_values(arg_keys[6], (N_LAT, N_LON, N_LON, CAP, K), K ** -0.5, 0.25, ((0, 4), (1, 128)), jnp.float32)
    obs_value = normal_values(arg_keys[7], (N_LAT, N_LON, N_LON, CAP), 1.0, 6.0, ((0, 4), (1, 128)), jnp.float32)
    obs_weight = jnp.clip(jnp.exp(math.log(5.0) - 2.3025851 * jax.random.uniform(arg_keys[8], (N_LAT, N_LON, N_LON, CAP), jnp.float32) ** block_levels(arg_keys[8], (N_LAT, N_LON, N_LON, CAP), ((0, 4), (1, 128)), -0.2, 0.2)), 0.5, 5.0)
    return {"moisture": moisture, "conductance": conductance, "inverse": inverse, "crop_mask": crop_mask, "adjoint_in": adjoint_in, "foot_anchor": foot_anchor, "antenna_gain": antenna_gain, "obs_value": obs_value, "obs_weight": obs_weight}


def stencil(field):
    padded = jnp.pad(field, ((0, 0), (1, 1), (1, 1)))
    return padded[:, 2:, 1:-1] + padded[:, :-2, 1:-1] + padded[:, 1:-1, 2:] + padded[:, 1:-1, :-2] - 4.0 * field


def columns(inverse, field, transpose):
    levels, height, breadth = field.shape
    blocks = inverse.shape[1]
    matrices = inverse.reshape(height, blocks, levels, levels)
    grouped = field.reshape(levels, height, blocks, breadth // blocks)
    form = "rbji,jrbc->irbc" if transpose else "rbij,jrbc->irbc"
    return jnp.einsum(form, matrices, grouped, precision=lax.Precision.HIGHEST).reshape(levels, height, breadth)


def reference(moisture, conductance, inverse, crop_mask, adjoint_in, foot_anchor, antenna_gain, obs_value, obs_weight):
    mask_float = crop_mask.astype(jnp.float32)
    deep = moisture[L - LG:]
    mixed = jnp.concatenate([moisture[:L - LG], deep + conductance * stencil(deep)], 0)
    solved = columns(inverse, mixed, False)
    topmost = solved[:LTOP] * mask_float
    live = (foot_anchor >= 0).astype(jnp.float32)
    anchor = jnp.maximum(foot_anchor, 0)
    lat_index = lax.broadcasted_iota(jnp.int32, foot_anchor.shape, 0)
    lon_index = lax.broadcasted_iota(jnp.int32, foot_anchor.shape, 1)
    row_at = (lat_index * CLAT + anchor // CLON).reshape(-1).astype(jnp.int32)
    col_at = (lon_index * CLON + anchor % CLON).reshape(-1).astype(jnp.int32)

    def one_window(row_start, col_start):
        return lax.dynamic_slice(topmost, (jnp.int32(0), row_start, col_start), (LTOP, FH, FW))

    window = jax.vmap(one_window)(row_at, col_at).reshape(foot_anchor.shape + (K,)) * live[..., None]
    window_owner = jnp.swapaxes(window, 1, 2)
    live_owner = jnp.swapaxes(live, 1, 2)
    predicted = jnp.sum(antenna_gain * window_owner, -1)
    residual = live_owner * obs_weight * (predicted - obs_value)
    back = jnp.swapaxes(residual[..., None] * antenna_gain, 1, 2).reshape(-1, LTOP, FH, FW)
    layer_at = jnp.arange(LTOP, dtype=jnp.int32)[None, :, None, None]
    rows_idx = row_at[:, None, None, None] + jnp.arange(FH, dtype=jnp.int32)[None, None, :, None]
    cols_idx = col_at[:, None, None, None] + jnp.arange(FW, dtype=jnp.int32)[None, None, None, :]
    topbar = jnp.zeros(topmost.shape, jnp.float32).at[layer_at, rows_idx, cols_idx].add(back)
    solvedbar = jnp.concatenate([adjoint_in[:LTOP] + topbar * mask_float, adjoint_in[LTOP:]], 0)
    mixedbar = columns(inverse, solvedbar, True)
    deepbar = mixedbar[L - LG:]
    gradient = jnp.concatenate([mixedbar[:L - LG], deepbar + stencil(conductance * deepbar)], 0)
    return gradient, residual
```

```python
import jax
import jax.numpy as jnp
from jax import lax
from jax.experimental import pallas as pl
from jax.experimental.pallas import tpu as pltpu
from jax.sharding import PartitionSpec as P

LG = 8
LTOP = 4
FH = 8
FW = 16
K = 512
LANES = 128


def neighbours(block, axis, dim):
    count = lax.axis_size(axis)
    forward = [(i, i + 1) for i in range(count - 1)]
    backward = [(target, source) for source, target in forward]
    size = block.shape[dim]
    low = lax.ppermute(lax.slice_in_dim(block, size - 1, size, axis=dim), axis, forward)
    high = lax.ppermute(lax.slice_in_dim(block, 0, 1, axis=dim), axis, backward)
    return low, high


def stencil(block):
    up, down = neighbours(block, "lat", 1)
    left, right = neighbours(block, "lon", 2)
    rows = block.shape[1]
    cols = block.shape[2]
    north = jnp.concatenate([up, lax.slice_in_dim(block, 0, rows - 1, axis=1)], 1)
    south = jnp.concatenate([lax.slice_in_dim(block, 1, rows, axis=1), down], 1)
    west = jnp.concatenate([left, lax.slice_in_dim(block, 0, cols - 1, axis=2)], 2)
    east = jnp.concatenate([lax.slice_in_dim(block, 1, cols, axis=2), right], 2)
    return north + south + west + east - 4.0 * block


def columns(matrices, field, transpose):
    levels, height, breadth = field.shape
    blocks = matrices.shape[1]
    grouped = field.reshape(levels, height, blocks, breadth // blocks)
    form = "rbji,jrbc->irbc" if transpose else "rbij,jrbc->irbc"
    out = jnp.einsum(form, matrices, grouped, precision=lax.Precision.HIGHEST)
    return out.reshape(out.shape[0], height, breadth)


def slot_place(anchor_ref, s, tile_rows, tile_cols):
    o = jnp.maximum(anchor_ref[s], 0)
    r = jnp.minimum(o // tile_cols, tile_rows - FH)
    c = jnp.minimum(o % tile_cols, tile_cols - FW)
    g0 = pl.multiple_of(jnp.minimum(r // FH, tile_rows // FH - 2) * FH, FH)
    return g0, r - g0, c


def placed_gain(gain_ref, s, off, c, tile_cols):
    g = gain_ref[s]
    g = pltpu.roll(g, off % FH, 1)
    g = pltpu.roll(g, c % LANES, 2)
    g = jnp.concatenate([g, g], axis=1)
    g = jnp.concatenate([g] * (tile_cols // LANES), axis=2)
    row = lax.broadcasted_iota(jnp.int32, g.shape, 1)
    lane = lax.broadcasted_iota(jnp.int32, g.shape, 2)
    inside = (row >= off) & (row < off + FH) & (lane >= c) & (lane < c + FW)
    return jnp.where(inside, g, 0.0)


def predict_kernel(anchor_ref, top_ref, gain_ref, out_ref):
    _, tile_rows, tile_cols = top_ref.shape
    slots = gain_ref.shape[0]

    def body(s, carry):
        g0, off, c = slot_place(anchor_ref, s, tile_rows, tile_cols)
        g = placed_gain(gain_ref, s, off, c, tile_cols)
        t = top_ref[:, pl.ds(g0, 2 * FH), :]
        part = jnp.sum(g * t, axis=0)
        part = part[:FH] + part[FH:]
        acc = part[:, 0:LANES]
        for q in range(1, tile_cols // LANES):
            acc = acc + part[:, q * LANES:(q + 1) * LANES]
        out_ref[s] = acc
        return carry

    lax.fori_loop(0, slots, body, 0, unroll=4)


def scatter_kernel(anchor_ref, res_ref, gain_ref, out_ref):
    _, tile_rows, tile_cols = out_ref.shape
    slots = gain_ref.shape[0]
    out_ref[...] = jnp.zeros(out_ref.shape, out_ref.dtype)

    def body(s, carry):
        g0, off, c = slot_place(anchor_ref, s, tile_rows, tile_cols)
        g = placed_gain(gain_ref, s, off, c, tile_cols)
        out_ref[:, pl.ds(g0, 2 * FH), :] += res_ref[s] * g
        return carry

    lax.fori_loop(0, slots, body, 0, unroll=4)


def predict(anchor, top, gain):
    slots = gain.shape[0]
    return pl.pallas_call(
        predict_kernel,
        out_shape=jax.ShapeDtypeStruct((slots, FH, LANES), jnp.float32),
        in_specs=[
            pl.BlockSpec(memory_space=pltpu.SMEM),
            pl.BlockSpec(memory_space=pltpu.VMEM),
            pl.BlockSpec(memory_space=pltpu.VMEM),
        ],
        out_specs=pl.BlockSpec(memory_space=pltpu.VMEM),
    )(anchor, top, gain)


def scatter(anchor, res, gain, top_shape):
    return pl.pallas_call(
        scatter_kernel,
        out_shape=jax.ShapeDtypeStruct(top_shape, jnp.float32),
        in_specs=[
            pl.BlockSpec(memory_space=pltpu.SMEM),
            pl.BlockSpec(memory_space=pltpu.SMEM),
            pl.BlockSpec(memory_space=pltpu.VMEM),
        ],
        out_specs=pl.BlockSpec(memory_space=pltpu.VMEM),
    )(anchor, res, gain)


def per_device(
    moisture,
    conductance,
    inverse,
    crop_mask,
    adjoint_in,
    foot_anchor,
    antenna_gain,
    obs_value,
    obs_weight,
):
    levels, tile_rows, tile_cols = moisture.shape
    mask_float = crop_mask.astype(jnp.float32)
    blocks = inverse.shape[1]
    matrices = inverse.reshape(tile_rows, blocks, levels, levels)

    owner_gain = antenna_gain[0, 0]
    owners, slots_per, _ = owner_gain.shape
    packed = jnp.concatenate(
        [owner_gain, obs_value[0, 0][..., None], obs_weight[0, 0][..., None]], -1
    )
    received = lax.all_to_all(packed, "lon", split_axis=0, concat_axis=0, tiled=True)
    slots = owners * slots_per
    gain = received[..., :K].reshape(slots, LTOP, FH, FW)
    gain = jnp.pad(gain, ((0, 0), (0, 0), (0, 0), (0, LANES - FW)))
    value = received[..., K].reshape(slots)
    weight = received[..., K + 1].reshape(slots)

    deep = moisture[levels - LG :]
    mixed = jnp.concatenate(
        [moisture[: levels - LG], deep + conductance * stencil(deep)], 0
    )
    solved_top = columns(matrices[:, :, :LTOP, :], mixed, False)
    topmost = solved_top * mask_float

    slot_anchor = foot_anchor[0, 0].reshape(slots)
    live = (slot_anchor >= 0).astype(jnp.float32)
    parts = predict(slot_anchor, topmost, gain)
    predicted = jnp.sum(parts, axis=(1, 2))
    residual = live * weight * (predicted - value)
    residual_out = lax.all_to_all(
        residual.reshape(owners, slots_per), "lon", split_axis=0, concat_axis=0, tiled=True
    )

    base = columns(matrices, adjoint_in, True)
    topbar = scatter(slot_anchor, residual, gain, topmost.shape) * mask_float
    mixedbar = base + columns(matrices[:, :, :LTOP, :], topbar, True)
    deepbar = mixedbar[levels - LG :]
    gradient = jnp.concatenate(
        [mixedbar[: levels - LG], deepbar + stencil(conductance * deepbar)], 0
    )
    return gradient, residual_out[None, None]


def solution(mesh):
    in_specs = (
        P(None, "lat", "lon"),
        P("lat", "lon"),
        P("lat", "lon", None),
        P("lat", "lon"),
        P(None, "lat", "lon"),
        P("lat", "lon", None, None),
        P("lat", "lon", None, None, None),
        P("lat", "lon", None, None),
        P("lat", "lon", None, None),
    )
    out_specs = (P(None, "lat", "lon"), P("lat", "lon", None, None))
    return jax.shard_map(
        per_device, mesh=mesh, in_specs=in_specs, out_specs=out_specs, check_vma=False
    )
```

```python
import jax
import jax.numpy as jnp
from jax import lax
from jax.experimental import pallas as pl
from jax.experimental.pallas import tpu as pltpu
from jax.sharding import PartitionSpec as P

LG = 8
LTOP = 4
FH = 8
FW = 16
K = 512
LANES = 128


def neighbours(block, axis, dim):
    count = lax.axis_size(axis)
    forward = [(i, i + 1) for i in range(count - 1)]
    backward = [(target, source) for source, target in forward]
    size = block.shape[dim]
    low = lax.ppermute(lax.slice_in_dim(block, size - 1, size, axis=dim), axis, forward)
    high = lax.ppermute(lax.slice_in_dim(block, 0, 1, axis=dim), axis, backward)
    return low, high


def stencil(block):
    up, down = neighbours(block, "lat", 1)
    left, right = neighbours(block, "lon", 2)
    rows = block.shape[1]
    cols = block.shape[2]
    north = jnp.concatenate([up, lax.slice_in_dim(block, 0, rows - 1, axis=1)], 1)
    south = jnp.concatenate([lax.slice_in_dim(block, 1, rows, axis=1), down], 1)
    west = jnp.concatenate([left, lax.slice_in_dim(block, 0, cols - 1, axis=2)], 2)
    east = jnp.concatenate([lax.slice_in_dim(block, 1, cols, axis=2), right], 2)
    return north + south + west + east - 4.0 * block


def columns(matrices, field, transpose):
    levels, height, breadth = field.shape
    blocks = matrices.shape[1]
    grouped = field.reshape(levels, height, blocks, breadth // blocks)
    form = "rbji,jrbc->irbc" if transpose else "rbij,jrbc->irbc"
    out = jnp.einsum(form, matrices, grouped, precision=lax.Precision.HIGHEST)
    return out.reshape(out.shape[0], height, breadth)


def footprint_kernel(anchor_ref, value_ref, weight_ref, top_ref, gain_ref, bar_ref, res_ref):
    layers, tile_rows, tile_cols = top_ref.shape
    slots = gain_ref.shape[0]
    groups = tile_cols // LANES
    bar_ref[...] = jnp.zeros(bar_ref.shape, bar_ref.dtype)
    row = lax.broadcasted_iota(jnp.int32, (2 * FH, tile_cols), 0)
    lane = lax.broadcasted_iota(jnp.int32, (2 * FH, tile_cols), 1)

    def body(s, carry):
        raw = anchor_ref[s]
        o = jnp.maximum(raw, 0)
        r = jnp.minimum(lax.div(o, tile_cols), tile_rows - FH)
        c = jnp.minimum(lax.rem(o, tile_cols), tile_cols - FW)
        flip = tile_rows - FH - r
        g0 = jnp.minimum(lax.div(flip, FH), tile_rows // FH - 2) * FH
        g0 = pl.multiple_of(g0, FH)
        off = flip - g0
        g = gain_ref[s]
        g = jnp.broadcast_to(g[:, None, :], (layers, FH, LANES))
        g = pltpu.roll(g, 0, 2, stride=FW, stride_axis=1)
        g = pltpu.roll(g, lax.rem(c + FW, LANES), 2)
        g = pltpu.roll(g, lax.rem(off, FH), 1)
        g = jnp.concatenate([g, g], axis=1)
        g = jnp.concatenate([g] * groups, axis=2)
        inside = (row >= off) & (row < off + FH) & (lane >= c) & (lane < c + FW)
        g = jnp.where(inside[None], g, 0.0)
        t = top_ref[:, pl.ds(g0, 2 * FH), :]
        part = jnp.sum(g * t, axis=0)
        part = part[:FH] + part[FH:]
        acc = part[:, 0:LANES]
        for q in range(1, groups):
            acc = acc + part[:, q * LANES:(q + 1) * LANES]
        predicted = jnp.sum(acc, axis=(0, 1), keepdims=True)
        live = jnp.where(raw >= 0, 1.0, 0.0).astype(jnp.float32)
        res = (live * weight_ref[s]) * (predicted - value_ref[s])
        res_ref[s] = jnp.broadcast_to(res, (FH, LANES))
        bar_ref[:, pl.ds(g0, 2 * FH), :] += res * g
        return carry

    lax.fori_loop(0, slots, body, 0, unroll=2)


def footprints(anchor, value, weight, top, gain):
    slots = gain.shape[0]
    smem = pl.BlockSpec(memory_space=pltpu.SMEM)
    vmem = pl.BlockSpec(memory_space=pltpu.VMEM)
    return pl.pallas_call(
        footprint_kernel,
        out_shape=(
            jax.ShapeDtypeStruct(top.shape, jnp.float32),
            jax.ShapeDtypeStruct((slots, FH, LANES), jnp.float32),
        ),
        in_specs=[smem, smem, smem, vmem, vmem],
        out_specs=(vmem, vmem),
    )(anchor, value, weight, top, gain)


def per_device(
    moisture,
    conductance,
    inverse,
    crop_mask,
    adjoint_in,
    foot_anchor,
    antenna_gain,
    obs_value,
    obs_weight,
):
    levels, tile_rows, tile_cols = moisture.shape
    mask_float = crop_mask.astype(jnp.float32)
    blocks = inverse.shape[1]
    matrices = inverse.reshape(tile_rows, blocks, levels, levels)

    owner_gain = antenna_gain[0, 0]
    owners, slots_per, _ = owner_gain.shape
    packed = jnp.concatenate(
        [owner_gain, obs_value[0, 0][..., None], obs_weight[0, 0][..., None]], -1
    )
    received = lax.all_to_all(packed, "lon", split_axis=0, concat_axis=0, tiled=True)
    slots = owners * slots_per
    gain = received[..., :K].reshape(slots, LTOP, LANES)
    value = received[..., K].reshape(slots)
    weight = received[..., K + 1].reshape(slots)

    deep = moisture[levels - LG :]
    mixed = jnp.concatenate(
        [moisture[: levels - LG], deep + conductance * stencil(deep)], 0
    )
    solved_top = columns(matrices[:, :, :LTOP, :], mixed, False)
    topmost = jnp.flip(solved_top * mask_float, 1)

    slot_anchor = foot_anchor[0, 0].reshape(slots)
    bar, rows = footprints(slot_anchor, value, weight, topmost, gain)
    residual = rows[:, 0, 0].reshape(owners, slots_per)
    residual_out = lax.all_to_all(residual, "lon", split_axis=0, concat_axis=0, tiled=True)

    base = columns(matrices, adjoint_in, True)
    topbar = jnp.flip(bar, 1) * mask_float
    mixedbar = base + columns(matrices[:, :, :LTOP, :], topbar, True)
    deepbar = mixedbar[levels - LG :]
    gradient = jnp.concatenate(
        [mixedbar[: levels - LG], deepbar + stencil(conductance * deepbar)], 0
    )
    return gradient, residual_out[None, None]


def solution(mesh):
    in_specs = (
        P(None, "lat", "lon"),
        P("lat", "lon"),
        P("lat", "lon", None),
        P("lat", "lon"),
        P(None, "lat", "lon"),
        P("lat", "lon", None, None),
        P("lat", "lon", None, None, None),
        P("lat", "lon", None, None),
        P("lat", "lon", None, None),
    )
    out_specs = (P(None, "lat", "lon"), P("lat", "lon", None, None))
    return jax.shard_map(
        per_device, mesh=mesh, in_specs=in_specs, out_specs=out_specs, check_vma=False
    )
```

```python
import jax
import jax.numpy as jnp
from jax import lax
from jax.experimental import pallas as pl
from jax.experimental.pallas import tpu as pltpu
from jax.sharding import PartitionSpec as P

LG = 8
LTOP = 4
FH = 8
FW = 16
K = 512
LANES = 128


def neighbours(edge_low, edge_high, axis):
    count = lax.axis_size(axis)
    forward = [(i, i + 1) for i in range(count - 1)]
    backward = [(target, source) for source, target in forward]
    return lax.ppermute(edge_high, axis, forward), lax.ppermute(edge_low, axis, backward)


def stencil(block):
    rows = block.shape[1]
    cols = block.shape[2]
    up, down = neighbours(block[:, 0:1, :], block[:, rows - 1 : rows, :], "lat")
    left, right = neighbours(block[:, :, 0], block[:, :, cols - 1], "lon")
    north = jnp.concatenate([up, lax.slice_in_dim(block, 0, rows - 1, axis=1)], 1)
    south = jnp.concatenate([lax.slice_in_dim(block, 1, rows, axis=1), down], 1)
    west = jnp.concatenate([left[:, :, None], lax.slice_in_dim(block, 0, cols - 1, axis=2)], 2)
    east = jnp.concatenate([lax.slice_in_dim(block, 1, cols, axis=2), right[:, :, None]], 2)
    return north + south + west + east - 4.0 * block


def columns(matrices, field, transpose):
    levels, height, breadth = field.shape
    blocks = matrices.shape[1]
    grouped = field.reshape(levels, height, blocks, breadth // blocks)
    form = "rbji,jrbc->irbc" if transpose else "rbij,jrbc->irbc"
    out = jnp.einsum(form, matrices, grouped, precision=lax.Precision.HIGHEST)
    return out.reshape(out.shape[0], height, breadth)


def footprint_kernel(anchor_ref, value_ref, weight_ref, top_ref, gain_ref, bar_ref, res_ref):
    layers, tile_rows, tile_cols = top_ref.shape
    slots = gain_ref.shape[0]
    groups = tile_cols // LANES
    row = lax.broadcasted_iota(jnp.int32, (2 * FH, tile_cols), 0)
    lane = lax.broadcasted_iota(jnp.int32, (2 * FH, tile_cols), 1)

    def placed(s):
        o = jnp.maximum(anchor_ref[s], 0)
        r = jnp.minimum(lax.div(o, tile_cols), tile_rows - FH)
        c = jnp.minimum(lax.rem(o, tile_cols), tile_cols - FW)
        flip = tile_rows - FH - r
        g0 = jnp.minimum(lax.div(flip, FH), tile_rows // FH - 2) * FH
        g0 = pl.multiple_of(g0, FH)
        off = flip - g0
        g = gain_ref[s]
        g = jnp.broadcast_to(g[:, None, :], (layers, FH, LANES))
        g = pltpu.roll(g, 0, 2, stride=FW, stride_axis=1)
        g = pltpu.roll(g, lax.rem(c + FW, LANES), 2)
        g = pltpu.roll(g, lax.rem(off, FH), 1)
        g = jnp.concatenate([g, g], axis=1)
        g = jnp.concatenate([g] * groups, axis=2)
        inside = (row >= off) & (row < off + FH) & (lane >= c) & (lane < c + FW)
        return g0, jnp.where(inside[None], g, 0.0)

    def predict(s, carry):
        g0, g = placed(s)
        t = top_ref[:, pl.ds(g0, 2 * FH), :]
        part = jnp.sum(g * t, axis=0)
        part = part[:FH] + part[FH:]
        acc = part[:, 0:LANES]
        for q in range(1, groups):
            acc = acc + part[:, q * LANES:(q + 1) * LANES]
        predicted = jnp.sum(acc, axis=(0, 1), keepdims=True)
        live = jnp.where(anchor_ref[s] >= 0, 1.0, 0.0).astype(jnp.float32)
        res = (live * weight_ref[s]) * (predicted - value_ref[s])
        res_ref[s] = jnp.broadcast_to(res, (FH, LANES))
        return carry

    def scatter(s, carry):
        g0, g = placed(s)
        res = res_ref[s][0:1, 0:1]
        bar_ref[:, pl.ds(g0, 2 * FH), :] += res * g
        return carry

    lax.fori_loop(0, slots, predict, 0, unroll=4)
    bar_ref[...] = jnp.zeros(bar_ref.shape, bar_ref.dtype)
    lax.fori_loop(0, slots, scatter, 0, unroll=4)


def footprints(anchor, value, weight, top, gain):
    slots = gain.shape[0]
    smem = pl.BlockSpec(memory_space=pltpu.SMEM)
    vmem = pl.BlockSpec(memory_space=pltpu.VMEM)
    return pl.pallas_call(
        footprint_kernel,
        out_shape=(
            jax.ShapeDtypeStruct(top.shape, jnp.float32),
            jax.ShapeDtypeStruct((slots, FH, LANES), jnp.float32),
        ),
        in_specs=[smem, smem, smem, vmem, vmem],
        out_specs=(vmem, vmem),
    )(anchor, value, weight, top, gain)


def per_device(
    moisture,
    conductance,
    inverse,
    crop_mask,
    adjoint_in,
    foot_anchor,
    antenna_gain,
    obs_value,
    obs_weight,
):
    levels, tile_rows, tile_cols = moisture.shape
    mask_float = crop_mask.astype(jnp.float32)
    blocks = inverse.shape[1]
    matrices = inverse.reshape(tile_rows, blocks, levels, levels)

    owner_gain = antenna_gain[0, 0]
    owners, slots_per, _ = owner_gain.shape
    packed = jnp.concatenate(
        [owner_gain, obs_value[0, 0][..., None], obs_weight[0, 0][..., None]], -1
    )
    received = lax.all_to_all(packed, "lon", split_axis=0, concat_axis=0, tiled=True)
    slots = owners * slots_per
    gain = received[..., :K].reshape(slots, LTOP, LANES)
    value = received[..., K].reshape(slots)
    weight = received[..., K + 1].reshape(slots)

    deep = moisture[levels - LG :]
    mixed = jnp.concatenate(
        [moisture[: levels - LG], deep + conductance * stencil(deep)], 0
    )
    solved_top = columns(matrices[:, :, :LTOP, :], mixed, False)
    topmost = jnp.flip(solved_top * mask_float, 1)

    slot_anchor = foot_anchor[0, 0].reshape(slots)
    bar, rows = footprints(slot_anchor, value, weight, topmost, gain)
    residual = rows[:, 0, 0].reshape(owners, slots_per)
    residual_out = lax.all_to_all(residual, "lon", split_axis=0, concat_axis=0, tiled=True)

    base = columns(matrices, adjoint_in, True)
    topbar = jnp.flip(bar, 1) * mask_float
    mixedbar = base + columns(matrices[:, :, :LTOP, :], topbar, True)
    deepbar = mixedbar[levels - LG :]
    gradient = jnp.concatenate(
        [mixedbar[: levels - LG], deepbar + stencil(conductance * deepbar)], 0
    )
    return gradient, residual_out[None, None]


def solution(mesh):
    in_specs = (
        P(None, "lat", "lon"),
        P("lat", "lon"),
        P("lat", "lon", None),
        P("lat", "lon"),
        P(None, "lat", "lon"),
        P("lat", "lon", None, None),
        P("lat", "lon", None, None, None),
        P("lat", "lon", None, None),
        P("lat", "lon", None, None),
    )
    out_specs = (P(None, "lat", "lon"), P("lat", "lon", None, None))
    return jax.shard_map(
        per_device, mesh=mesh, in_specs=in_specs, out_specs=out_specs, check_vma=False
    )
```

```python
import jax
import jax.numpy as jnp
from jax import lax
from jax.experimental import pallas as pl
from jax.experimental.pallas import tpu as pltpu
from jax.sharding import PartitionSpec as P

LG = 8
LTOP = 4
FH = 8
FW = 16
K = 512
LANES = 128


def neighbours(edge_low, edge_high, axis):
    count = lax.axis_size(axis)
    forward = [(i, i + 1) for i in range(count - 1)]
    backward = [(target, source) for source, target in forward]
    return lax.ppermute(edge_high, axis, forward), lax.ppermute(edge_low, axis, backward)


def stencil(block):
    rows = block.shape[1]
    cols = block.shape[2]
    up, down = neighbours(block[:, 0:1, :], block[:, rows - 1 : rows, :], "lat")
    left, right = neighbours(block[:, :, 0], block[:, :, cols - 1], "lon")
    north = jnp.concatenate([up, lax.slice_in_dim(block, 0, rows - 1, axis=1)], 1)
    south = jnp.concatenate([lax.slice_in_dim(block, 1, rows, axis=1), down], 1)
    west = jnp.concatenate([left[:, :, None], lax.slice_in_dim(block, 0, cols - 1, axis=2)], 2)
    east = jnp.concatenate([lax.slice_in_dim(block, 1, cols, axis=2), right[:, :, None]], 2)
    return north + south + west + east - 4.0 * block


def columns(matrices, field, transpose):
    levels, height, breadth = field.shape
    blocks = matrices.shape[1]
    grouped = field.reshape(levels, height, blocks, breadth // blocks)
    form = "rbji,jrbc->irbc" if transpose else "rbij,jrbc->irbc"
    out = jnp.einsum(form, matrices, grouped, precision=lax.Precision.HIGHEST)
    return out.reshape(out.shape[0], height, breadth)


def footprint_kernel(anchor_ref, value_ref, weight_ref, top_ref, gain_ref, bar_ref, res_ref):
    tile_cols, wide = top_ref.shape
    slots = gain_ref.shape[0]
    tile_rows = wide // LTOP
    span = FW + FH
    sub = lax.broadcasted_iota(jnp.int32, (FH, wide), 0)

    def placed(s):
        o = jnp.maximum(anchor_ref[s], 0)
        r = jnp.minimum(lax.div(o, tile_cols), tile_rows - FH)
        c = jnp.minimum(lax.rem(o, tile_cols), tile_cols - FW)
        c8 = pl.multiple_of(jnp.minimum(lax.div(c, FH) * FH, tile_cols - span), FH)
        off = c - c8
        g = pltpu.roll(gain_ref[s], r, 1)
        a = pltpu.roll(g[0:FH], lax.rem(off, FH), 0)
        b = pltpu.roll(g[FH:FW], lax.rem(off, FH), 0)
        low = sub >= off
        parts = (jnp.where(low, a, 0.0), jnp.where(low, b, a), jnp.where(low, 0.0, b))
        return c8, parts

    def predict(s, carry):
        c8, parts = placed(s)
        t = top_ref[pl.ds(c8, span), :]
        acc = parts[0] * t[0:FH] + parts[1] * t[FH:FW] + parts[2] * t[FW:span]
        predicted = jnp.sum(acc, axis=(0, 1), keepdims=True)
        live = jnp.where(anchor_ref[s] >= 0, 1.0, 0.0).astype(jnp.float32)
        res = (live * weight_ref[s]) * (predicted - value_ref[s])
        res_ref[s] = jnp.broadcast_to(res, (FH, LANES))
        return carry

    def scatter(s, carry):
        c8, parts = placed(s)
        res = res_ref[s][0:1, 0:1]
        bar_ref[pl.ds(c8, span), :] += res * jnp.concatenate(parts, axis=0)
        return carry

    lax.fori_loop(0, slots, predict, 0, unroll=8)
    bar_ref[...] = jnp.zeros(bar_ref.shape, bar_ref.dtype)
    lax.fori_loop(0, slots, scatter, 0, unroll=8)


def footprints(anchor, value, weight, top, gain):
    slots = gain.shape[0]
    smem = pl.BlockSpec(memory_space=pltpu.SMEM)
    vmem = pl.BlockSpec(memory_space=pltpu.VMEM)
    return pl.pallas_call(
        footprint_kernel,
        out_shape=(
            jax.ShapeDtypeStruct(top.shape, jnp.float32),
            jax.ShapeDtypeStruct((slots, FH, LANES), jnp.float32),
        ),
        in_specs=[smem, smem, smem, vmem, vmem],
        out_specs=(vmem, vmem),
    )(anchor, value, weight, top, gain)


def per_device(
    moisture,
    conductance,
    inverse,
    crop_mask,
    adjoint_in,
    foot_anchor,
    antenna_gain,
    obs_value,
    obs_weight,
):
    levels, tile_rows, tile_cols = moisture.shape
    mask_float = crop_mask.astype(jnp.float32)
    blocks = inverse.shape[1]
    matrices = inverse.reshape(tile_rows, blocks, levels, levels)

    owner_gain = antenna_gain[0, 0]
    owners, slots_per, _ = owner_gain.shape
    packed = jnp.concatenate(
        [owner_gain, obs_value[0, 0][..., None], obs_weight[0, 0][..., None]], -1
    )
    received = lax.all_to_all(packed, "lon", split_axis=0, concat_axis=0, tiled=True)
    slots = owners * slots_per
    gain = received[..., :K].reshape(slots, LTOP, FH, FW).transpose(0, 3, 1, 2)
    gain = jnp.pad(gain, ((0, 0), (0, 0), (0, 0), (0, tile_rows - FH)))
    gain = gain.reshape(slots, FW, LTOP * tile_rows)
    value = received[..., K].reshape(slots)
    weight = received[..., K + 1].reshape(slots)

    deep = moisture[levels - LG :]
    mixed = jnp.concatenate(
        [moisture[: levels - LG], deep + conductance * stencil(deep)], 0
    )
    solved_top = columns(matrices[:, :, :LTOP, :], mixed, False)
    topmost = (solved_top * mask_float).transpose(2, 0, 1).reshape(tile_cols, LTOP * tile_rows)

    slot_anchor = foot_anchor[0, 0].reshape(slots)
    bar, rows = footprints(slot_anchor, value, weight, topmost, gain)
    residual = rows[:, 0, 0].reshape(owners, slots_per)
    residual_out = lax.all_to_all(residual, "lon", split_axis=0, concat_axis=0, tiled=True)

    base = columns(matrices, adjoint_in, True)
    topbar = bar.reshape(tile_cols, LTOP, tile_rows).transpose(1, 2, 0) * mask_float
    mixedbar = base + columns(matrices[:, :, :LTOP, :], topbar, True)
    deepbar = mixedbar[levels - LG :]
    gradient = jnp.concatenate(
        [mixedbar[: levels - LG], deepbar + stencil(conductance * deepbar)], 0
    )
    return gradient, residual_out[None, None]


def solution(mesh):
    in_specs = (
        P(None, "lat", "lon"),
        P("lat", "lon"),
        P("lat", "lon", None),
        P("lat", "lon"),
        P(None, "lat", "lon"),
        P("lat", "lon", None, None),
        P("lat", "lon", None, None, None),
        P("lat", "lon", None, None),
        P("lat", "lon", None, None),
    )
    out_specs = (P(None, "lat", "lon"), P("lat", "lon", None, None))
    return jax.shard_map(
        per_device, mesh=mesh, in_specs=in_specs, out_specs=out_specs, check_vma=False
    )
```

```python
import jax
import jax.numpy as jnp
from jax import lax
from jax.experimental import pallas as pl
from jax.experimental.pallas import tpu as pltpu
from jax.sharding import PartitionSpec as P

LG = 8
LTOP = 4
FH = 8
FW = 16
K = 512
LANES = 128


def neighbours(edge_low, edge_high, axis):
    count = lax.axis_size(axis)
    forward = [(i, i + 1) for i in range(count - 1)]
    backward = [(target, source) for source, target in forward]
    return lax.ppermute(edge_high, axis, forward), lax.ppermute(edge_low, axis, backward)


def stencil(block):
    rows = block.shape[1]
    cols = block.shape[2]
    up, down = neighbours(block[:, 0:1, :], block[:, rows - 1 : rows, :], "lat")
    left, right = neighbours(block[:, :, 0], block[:, :, cols - 1], "lon")
    north = jnp.concatenate([up, lax.slice_in_dim(block, 0, rows - 1, axis=1)], 1)
    south = jnp.concatenate([lax.slice_in_dim(block, 1, rows, axis=1), down], 1)
    west = jnp.concatenate([left[:, :, None], lax.slice_in_dim(block, 0, cols - 1, axis=2)], 2)
    east = jnp.concatenate([lax.slice_in_dim(block, 1, cols, axis=2), right[:, :, None]], 2)
    return north + south + west + east - 4.0 * block


def columns(matrices, field, transpose):
    levels, height, breadth = field.shape
    blocks = matrices.shape[1]
    grouped = field.reshape(levels, height, blocks, breadth // blocks)
    form = "rbji,jrbc->irbc" if transpose else "rbij,jrbc->irbc"
    out = jnp.einsum(form, matrices, grouped, precision=lax.Precision.HIGHEST)
    return out.reshape(out.shape[0], height, breadth)


def footprint_kernel(anchor_ref, value_ref, weight_ref, top_ref, gain_ref, bar_ref, res_ref):
    tile_cols, wide = top_ref.shape
    slots, _, narrow = gain_ref.shape
    tile_rows = wide // LTOP
    span = FW + FH
    sub = lax.broadcasted_iota(jnp.int32, (FH, wide), 0)
    pad = jnp.zeros((FW, wide - narrow), jnp.float32)

    def placed(s):
        o = jnp.maximum(anchor_ref[s], 0)
        r = jnp.minimum(lax.div(o, tile_cols), tile_rows - FH)
        c = jnp.minimum(lax.rem(o, tile_cols), tile_cols - FW)
        c8 = pl.multiple_of(jnp.minimum(lax.div(c, FH) * FH, tile_cols - span), FH)
        off = c - c8
        g = jnp.concatenate([gain_ref[s], pad], axis=1)
        g = pltpu.roll(g, r * LTOP, 1)
        a = pltpu.roll(g[0:FH], lax.rem(off, FH), 0)
        b = pltpu.roll(g[FH:FW], lax.rem(off, FH), 0)
        low = sub >= off
        parts = (jnp.where(low, a, 0.0), jnp.where(low, b, a), jnp.where(low, 0.0, b))
        return c8, parts

    def predict(s, carry):
        c8, parts = placed(s)
        t = top_ref[pl.ds(c8, span), :]
        acc = parts[0] * t[0:FH] + parts[1] * t[FH:FW] + parts[2] * t[FW:span]
        predicted = jnp.sum(acc, axis=(0, 1), keepdims=True)
        live = jnp.where(anchor_ref[s] >= 0, 1.0, 0.0).astype(jnp.float32)
        res = (live * weight_ref[s]) * (predicted - value_ref[s])
        res_ref[s] = jnp.broadcast_to(res, (FH, LANES))
        return carry

    def scatter(s, carry):
        c8, parts = placed(s)
        res = res_ref[s][0:1, 0:1]
        bar_ref[pl.ds(c8, span), :] += res * jnp.concatenate(parts, axis=0)
        return carry

    lax.fori_loop(0, slots, predict, 0, unroll=8)
    bar_ref[...] = jnp.zeros(bar_ref.shape, bar_ref.dtype)
    lax.fori_loop(0, slots, scatter, 0, unroll=8)


def footprints(anchor, value, weight, top, gain):
    slots = gain.shape[0]
    smem = pl.BlockSpec(memory_space=pltpu.SMEM)
    vmem = pl.BlockSpec(memory_space=pltpu.VMEM)
    return pl.pallas_call(
        footprint_kernel,
        out_shape=(
            jax.ShapeDtypeStruct(top.shape, jnp.float32),
            jax.ShapeDtypeStruct((slots, FH, LANES), jnp.float32),
        ),
        in_specs=[smem, smem, smem, vmem, vmem],
        out_specs=(vmem, vmem),
    )(anchor, value, weight, top, gain)


def per_device(
    moisture,
    conductance,
    inverse,
    crop_mask,
    adjoint_in,
    foot_anchor,
    antenna_gain,
    obs_value,
    obs_weight,
):
    levels, tile_rows, tile_cols = moisture.shape
    mask_float = crop_mask.astype(jnp.float32)
    blocks = inverse.shape[1]
    matrices = inverse.reshape(tile_rows, blocks, levels, levels)

    owner_gain = antenna_gain[0, 0]
    owners, slots_per, _ = owner_gain.shape
    packed = jnp.concatenate(
        [owner_gain, obs_value[0, 0][..., None], obs_weight[0, 0][..., None]], -1
    )
    received = lax.all_to_all(packed, "lon", split_axis=0, concat_axis=0, tiled=True)
    slots = owners * slots_per
    source = lax.broadcasted_iota(jnp.int32, (K, K), 0)
    target = lax.broadcasted_iota(jnp.int32, (K, K), 1)
    layer_of = source // (FH * FW)
    row_of = (source // FW) % FH
    col_of = source % FW
    reorder = (target == (col_of * FH + row_of) * LTOP + layer_of).astype(jnp.float32)
    gain = jnp.dot(received[..., :K].reshape(slots, K), reorder, precision=lax.Precision.HIGHEST)
    gain = gain.reshape(slots, FW, FH * LTOP)
    value = received[..., K].reshape(slots)
    weight = received[..., K + 1].reshape(slots)

    deep = moisture[levels - LG :]
    mixed = jnp.concatenate(
        [moisture[: levels - LG], deep + conductance * stencil(deep)], 0
    )
    solved_top = columns(matrices[:, :, :LTOP, :], mixed, False)
    topmost = (solved_top * mask_float).transpose(2, 1, 0).reshape(tile_cols, tile_rows * LTOP)

    slot_anchor = foot_anchor[0, 0].reshape(slots)
    bar, rows = footprints(slot_anchor, value, weight, topmost, gain)
    residual = rows[:, 0, 0].reshape(owners, slots_per)
    residual_out = lax.all_to_all(residual, "lon", split_axis=0, concat_axis=0, tiled=True)

    base = columns(matrices, adjoint_in, True)
    topbar = bar.reshape(tile_cols, tile_rows, LTOP).transpose(2, 1, 0) * mask_float
    mixedbar = base + columns(matrices[:, :, :LTOP, :], topbar, True)
    deepbar = mixedbar[levels - LG :]
    gradient = jnp.concatenate(
        [mixedbar[: levels - LG], deepbar + stencil(conductance * deepbar)], 0
    )
    return gradient, residual_out[None, None]


def solution(mesh):
    in_specs = (
        P(None, "lat", "lon"),
        P("lat", "lon"),
        P("lat", "lon", None),
        P("lat", "lon"),
        P(None, "lat", "lon"),
        P("lat", "lon", None, None),
        P("lat", "lon", None, None, None),
        P("lat", "lon", None, None),
        P("lat", "lon", None, None),
    )
    out_specs = (P(None, "lat", "lon"), P("lat", "lon", None, None))
    return jax.shard_map(
        per_device, mesh=mesh, in_specs=in_specs, out_specs=out_specs, check_vma=False
    )
```

```python
import jax
import numpy as np
import jax.numpy as jnp
from jax import lax
from jax.experimental import pallas as pl
from jax.experimental.pallas import tpu as pltpu
from jax.sharding import PartitionSpec as P

LG = 8
LTOP = 4
FH = 8
FW = 16
K = 512
LANES = 128


def neighbours(edge_low, edge_high, axis):
    count = lax.axis_size(axis)
    forward = [(i, i + 1) for i in range(count - 1)]
    backward = [(target, source) for source, target in forward]
    return lax.ppermute(edge_high, axis, forward), lax.ppermute(edge_low, axis, backward)


def stencil(block):
    rows = block.shape[1]
    cols = block.shape[2]
    up, down = neighbours(block[:, 0:1, :], block[:, rows - 1 : rows, :], "lat")
    left, right = neighbours(block[:, :, 0], block[:, :, cols - 1], "lon")
    north = jnp.concatenate([up, lax.slice_in_dim(block, 0, rows - 1, axis=1)], 1)
    south = jnp.concatenate([lax.slice_in_dim(block, 1, rows, axis=1), down], 1)
    west = jnp.concatenate([left[:, :, None], lax.slice_in_dim(block, 0, cols - 1, axis=2)], 2)
    east = jnp.concatenate([lax.slice_in_dim(block, 1, cols, axis=2), right[:, :, None]], 2)
    return north + south + west + east - 4.0 * block


def columns(matrices, field, transpose):
    levels, height, breadth = field.shape
    blocks = matrices.shape[1]
    grouped = field.reshape(levels, height, blocks, breadth // blocks)
    form = "rbji,jrbc->irbc" if transpose else "rbij,jrbc->irbc"
    out = jnp.einsum(form, matrices, grouped, precision=lax.Precision.HIGHEST)
    return out.reshape(out.shape[0], height, breadth)


def window_gain(anchor_ref, gain_ref, s, tile_cols, tile_rows, sub, pad):
    span = FW + FH
    o = jnp.maximum(anchor_ref[s // 2, s % 2], 0)
    r = jnp.minimum(lax.div(o, tile_cols), tile_rows - FH)
    c = jnp.minimum(lax.rem(o, tile_cols), tile_cols - FW)
    c8 = pl.multiple_of(jnp.minimum(lax.div(c, FH) * FH, tile_cols - span), FH)
    off = c - c8
    g = jnp.concatenate([gain_ref[s], pad], axis=1)
    g = pltpu.roll(g, r * LTOP, 1)
    a = pltpu.roll(g[0:FH], lax.rem(off, FH), 0)
    b = pltpu.roll(g[FH:FW], lax.rem(off, FH), 0)
    low = sub >= off
    return c8, (jnp.where(low, a, 0.0), jnp.where(low, b, a), jnp.where(low, 0.0, b))


def predict_kernel(anchor_ref, obs_ref, top_ref, gain_ref, res_ref):
    tile_cols, wide = top_ref.shape
    _, _, narrow = gain_ref.shape
    tile_rows = wide // LTOP
    span = FW + FH
    sub = lax.broadcasted_iota(jnp.int32, (FH, wide), 0)
    pad = jnp.zeros((FW, wide - narrow), jnp.float32)

    def block(q, carry):
        out = jnp.zeros((FH, LANES), jnp.float32)
        for t in range(FH):
            s = q * FH + t
            c8, parts = window_gain(anchor_ref, gain_ref, s, tile_cols, tile_rows, sub, pad)
            win = top_ref[pl.ds(c8, span), :]
            acc = parts[0] * win[0:FH] + parts[1] * win[FH:FW] + parts[2] * win[FW:span]
            predicted = jnp.sum(acc, axis=(0, 1), keepdims=True)
            k = q * (FH // 2) + t // 2
            live = jnp.where(anchor_ref[k, t % 2] >= 0, 1.0, 0.0).astype(jnp.float32)
            res = (live * obs_ref[k, t % 2, 1]) * (predicted - obs_ref[k, t % 2, 0])
            out = jnp.where(sub[:, :LANES] == t, res, out)
        res_ref[q] = out
        return carry

    lax.fori_loop(0, res_ref.shape[0], block, 0)


def scatter_kernel(anchor_ref, res_ref, gain_ref, bar_ref):
    tile_cols, wide = bar_ref.shape
    _, _, narrow = gain_ref.shape
    tile_rows = wide // LTOP
    span = FW + FH
    sub = lax.broadcasted_iota(jnp.int32, (FH, wide), 0)
    pad = jnp.zeros((FW, wide - narrow), jnp.float32)
    bar_ref[...] = jnp.zeros(bar_ref.shape, bar_ref.dtype)

    def block(q, carry):
        res_block = res_ref[q]
        for t in range(FH):
            s = q * FH + t
            c8, parts = window_gain(anchor_ref, gain_ref, s, tile_cols, tile_rows, sub, pad)
            res = res_block[t:t + 1, 0:1]
            bar_ref[pl.ds(c8, span), :] += res * jnp.concatenate(parts, axis=0)
        return carry

    lax.fori_loop(0, res_ref.shape[0], block, 0)


def predict(anchor, obs, top, gain):
    slots = gain.shape[0]
    smem = pl.BlockSpec(memory_space=pltpu.SMEM)
    vmem = pl.BlockSpec(memory_space=pltpu.VMEM)
    return pl.pallas_call(
        predict_kernel,
        out_shape=jax.ShapeDtypeStruct((slots // FH, FH, LANES), jnp.float32),
        in_specs=[smem, smem, vmem, vmem],
        out_specs=vmem,
    )(anchor, obs, top, gain)


def scatter(anchor, res, gain, top_shape):
    smem = pl.BlockSpec(memory_space=pltpu.SMEM)
    vmem = pl.BlockSpec(memory_space=pltpu.VMEM)
    return pl.pallas_call(
        scatter_kernel,
        out_shape=jax.ShapeDtypeStruct(top_shape, jnp.float32),
        in_specs=[smem, vmem, vmem],
        out_specs=vmem,
    )(anchor, res, gain)


def reorder_matrix():
    source = np.arange(K)
    layer_of = source // (FH * FW)
    row_of = (source // FW) % FH
    col_of = source % FW
    matrix = np.zeros((K, K), np.float32)
    matrix[source, (col_of * FH + row_of) * LTOP + layer_of] = 1.0
    return matrix


def per_device(
    moisture,
    conductance,
    inverse,
    crop_mask,
    adjoint_in,
    foot_anchor,
    antenna_gain,
    obs_value,
    obs_weight,
):
    levels, tile_rows, tile_cols = moisture.shape
    mask_float = crop_mask.astype(jnp.float32)
    blocks = inverse.shape[1]
    matrices = inverse.reshape(tile_rows, blocks, levels, levels)

    owner_gain = antenna_gain[0, 0]
    owners, slots_per, _ = owner_gain.shape
    packed = jnp.concatenate(
        [owner_gain, obs_value[0, 0][..., None], obs_weight[0, 0][..., None]], -1
    )
    received = lax.all_to_all(packed, "lon", split_axis=0, concat_axis=0, tiled=True)
    slots = owners * slots_per
    gain = jnp.dot(
        received[..., :K].reshape(slots, K), jnp.asarray(reorder_matrix()), precision=lax.Precision.HIGHEST
    )
    gain = gain.reshape(slots, FW, FH * LTOP)
    obs = received[..., K : K + 2]

    deep = moisture[levels - LG :]
    mixed = jnp.concatenate(
        [moisture[: levels - LG], deep + conductance * stencil(deep)], 0
    )
    solved_top = columns(matrices[:, :, :LTOP, :], mixed, False)
    topmost = (solved_top * mask_float).transpose(2, 1, 0).reshape(tile_cols, tile_rows * LTOP)

    slot_anchor = foot_anchor[0, 0]
    res_rows = predict(slot_anchor, obs, topmost, gain)
    residual_out = lax.all_to_all(
        res_rows[:, :, 0].reshape(owners, slots_per), "lon", split_axis=0, concat_axis=0, tiled=True
    )

    base = columns(matrices, adjoint_in, True)
    bar = scatter(slot_anchor, res_rows, gain, topmost.shape)
    topbar = bar.reshape(tile_cols, tile_rows, LTOP).transpose(2, 1, 0) * mask_float
    mixedbar = base + columns(matrices[:, :, :LTOP, :], topbar, True)
    deepbar = mixedbar[levels - LG :]
    gradient = jnp.concatenate(
        [mixedbar[: levels - LG], deepbar + stencil(conductance * deepbar)], 0
    )
    return gradient, residual_out[None, None]


def solution(mesh):
    in_specs = (
        P(None, "lat", "lon"),
        P("lat", "lon"),
        P("lat", "lon", None),
        P("lat", "lon"),
        P(None, "lat", "lon"),
        P("lat", "lon", None, None),
        P("lat", "lon", None, None, None),
        P("lat", "lon", None, None),
        P("lat", "lon", None, None),
    )
    out_specs = (P(None, "lat", "lon"), P("lat", "lon", None, None))
    return jax.shard_map(
        per_device, mesh=mesh, in_specs=in_specs, out_specs=out_specs, check_vma=False
    )
```

```python
import jax
import numpy as np
import jax.numpy as jnp
from jax import lax
from jax.experimental import pallas as pl
from jax.experimental.pallas import tpu as pltpu
from jax.sharding import PartitionSpec as P

LG = 8
LTOP = 4
FH = 8
FW = 16
K = 512
LANES = 128


def neighbours(edge_low, edge_high, axis):
    count = lax.axis_size(axis)
    forward = [(i, i + 1) for i in range(count - 1)]
    backward = [(target, source) for source, target in forward]
    return lax.ppermute(edge_high, axis, forward), lax.ppermute(edge_low, axis, backward)


def stencil(block):
    rows = block.shape[1]
    cols = block.shape[2]
    up, down = neighbours(block[:, 0:1, :], block[:, rows - 1 : rows, :], "lat")
    left, right = neighbours(block[:, :, 0], block[:, :, cols - 1], "lon")
    north = jnp.concatenate([up, lax.slice_in_dim(block, 0, rows - 1, axis=1)], 1)
    south = jnp.concatenate([lax.slice_in_dim(block, 1, rows, axis=1), down], 1)
    west = jnp.concatenate([left[:, :, None], lax.slice_in_dim(block, 0, cols - 1, axis=2)], 2)
    east = jnp.concatenate([lax.slice_in_dim(block, 1, cols, axis=2), right[:, :, None]], 2)
    return north + south + west + east - 4.0 * block


def columns(matrices, field, transpose):
    levels, height, breadth = field.shape
    blocks = matrices.shape[1]
    grouped = field.reshape(levels, height, blocks, breadth // blocks)
    form = "rbji,jrbc->irbc" if transpose else "rbij,jrbc->irbc"
    out = jnp.einsum(form, matrices, grouped, precision=lax.Precision.HIGHEST)
    return out.reshape(out.shape[0], height, breadth)


def window_gain(anchor_ref, gain_ref, s, tile_cols, tile_rows, sub, pad):
    span = FW + FH
    o = jnp.maximum(anchor_ref[s // 2, s % 2], 0)
    r = jnp.minimum(lax.div(o, tile_cols), tile_rows - FH)
    c = jnp.minimum(lax.rem(o, tile_cols), tile_cols - FW)
    c8 = pl.multiple_of(jnp.minimum(lax.div(c, FH) * FH, tile_cols - span), FH)
    off = c - c8
    g = jnp.concatenate([gain_ref[s], pad], axis=1)
    g = pltpu.roll(g, r * LTOP, 1)
    a = pltpu.roll(g[0:FH], lax.rem(off, FH), 0)
    b = pltpu.roll(g[FH:FW], lax.rem(off, FH), 0)
    low = sub >= off
    return c8, (jnp.where(low, a, 0.0), jnp.where(low, b, a), jnp.where(low, 0.0, b))


def predict_kernel(anchor_ref, obs_ref, top_ref, gain_ref, res_ref):
    tile_cols, wide = top_ref.shape
    _, _, narrow = gain_ref.shape
    tile_rows = wide // LTOP
    span = FW + FH
    sub = lax.broadcasted_iota(jnp.int32, (FH, wide), 0)
    pad = jnp.zeros((FW, wide - narrow), jnp.float32)

    def block(q, carry):
        out = jnp.zeros((FH, LANES), jnp.float32)
        for t in range(FH):
            s = q * FH + t
            c8, parts = window_gain(anchor_ref, gain_ref, s, tile_cols, tile_rows, sub, pad)
            win = top_ref[pl.ds(c8, span), :]
            acc = parts[0] * win[0:FH] + parts[1] * win[FH:FW] + parts[2] * win[FW:span]
            predicted = jnp.sum(acc, axis=(0, 1), keepdims=True)
            k = q * (FH // 2) + t // 2
            live = jnp.where(anchor_ref[k, t % 2] >= 0, 1.0, 0.0).astype(jnp.float32)
            res = (live * obs_ref[k, t % 2, 1]) * (predicted - obs_ref[k, t % 2, 0])
            out = jnp.where(sub[:, :LANES] == t, res, out)
        res_ref[q] = out
        return carry

    lax.fori_loop(0, res_ref.shape[0], block, 0)


def scatter_kernel(anchor_ref, res_ref, gain_ref, bar_ref):
    tile_cols, wide = bar_ref.shape
    _, _, narrow = gain_ref.shape
    tile_rows = wide // LTOP
    span = FW + FH
    sub = lax.broadcasted_iota(jnp.int32, (FH, wide), 0)
    pad = jnp.zeros((FW, wide - narrow), jnp.float32)
    bar_ref[...] = jnp.zeros(bar_ref.shape, bar_ref.dtype)

    def block(q, carry):
        res_block = res_ref[q]
        for t in range(FH):
            s = q * FH + t
            c8, parts = window_gain(anchor_ref, gain_ref, s, tile_cols, tile_rows, sub, pad)
            res = res_block[t:t + 1, 0:1]
            bar_ref[pl.ds(c8, span), :] += res * jnp.concatenate(parts, axis=0)
        return carry

    lax.fori_loop(0, res_ref.shape[0], block, 0)


def predict(anchor, obs, top, gain):
    slots = gain.shape[0]
    smem = pl.BlockSpec(memory_space=pltpu.SMEM)
    vmem = pl.BlockSpec(memory_space=pltpu.VMEM)
    return pl.pallas_call(
        predict_kernel,
        out_shape=jax.ShapeDtypeStruct((slots // FH, FH, LANES), jnp.float32),
        in_specs=[smem, smem, vmem, vmem],
        out_specs=vmem,
    )(anchor, obs, top, gain)


def scatter(anchor, res, gain, top_shape):
    smem = pl.BlockSpec(memory_space=pltpu.SMEM)
    vmem = pl.BlockSpec(memory_space=pltpu.VMEM)
    return pl.pallas_call(
        scatter_kernel,
        out_shape=jax.ShapeDtypeStruct(top_shape, jnp.float32),
        in_specs=[smem, vmem, vmem],
        out_specs=vmem,
    )(anchor, res, gain)


def reorder_matrix():
    source = np.arange(K)
    layer_of = source // (FH * FW)
    row_of = (source // FW) % FH
    col_of = source % FW
    matrix = np.zeros((K, K), np.float32)
    matrix[source, (col_of * FH + row_of) * LTOP + layer_of] = 1.0
    return matrix


def per_device(
    moisture,
    conductance,
    inverse,
    crop_mask,
    adjoint_in,
    foot_anchor,
    antenna_gain,
    obs_value,
    obs_weight,
):
    levels, tile_rows, tile_cols = moisture.shape
    mask_float = crop_mask.astype(jnp.float32)
    blocks = inverse.shape[1]
    matrices = inverse.reshape(tile_rows, blocks, levels, levels)

    owner_gain = antenna_gain[0, 0]
    owners, slots_per, _ = owner_gain.shape
    packed = jnp.concatenate(
        [owner_gain, obs_value[0, 0][..., None], obs_weight[0, 0][..., None]], -1
    )
    received = lax.all_to_all(packed, "lon", split_axis=0, concat_axis=0, tiled=True)
    slots = owners * slots_per
    gain = jnp.dot(
        received[..., :K].reshape(slots, K), jnp.asarray(reorder_matrix()), precision=lax.Precision.HIGHEST
    )
    gain = gain.reshape(slots, FW, FH * LTOP)
    obs = received[..., K : K + 2]

    deep = moisture[levels - LG :]
    mixed = jnp.concatenate(
        [moisture[: levels - LG], deep + conductance * stencil(deep)], 0
    )
    solved_top = columns(matrices[:, :, :LTOP, :], mixed, False)
    topmost = (solved_top * mask_float).transpose(2, 1, 0).reshape(tile_cols, tile_rows * LTOP)

    slot_anchor = foot_anchor[0, 0]
    res_rows = predict(slot_anchor, obs, topmost, gain)
    residual = res_rows[:, :, 0].reshape(owners, 1, slots_per)
    column = lax.broadcasted_iota(jnp.int32, (1, owners, 1), 1) == lax.axis_index("lon")
    spread = jnp.where(column, residual, 0.0)
    residual_out = lax.psum_scatter(spread, "lon", scatter_dimension=0, tiled=True)[0]

    base = columns(matrices, adjoint_in, True)
    bar = scatter(slot_anchor, res_rows, gain, topmost.shape)
    topbar = bar.reshape(tile_cols, tile_rows, LTOP).transpose(2, 1, 0) * mask_float
    mixedbar = base + columns(matrices[:, :, :LTOP, :], topbar, True)
    deepbar = mixedbar[levels - LG :]
    gradient = jnp.concatenate(
        [mixedbar[: levels - LG], deepbar + stencil(conductance * deepbar)], 0
    )
    return gradient, residual_out[None, None]


def solution(mesh):
    in_specs = (
        P(None, "lat", "lon"),
        P("lat", "lon"),
        P("lat", "lon", None),
        P("lat", "lon"),
        P(None, "lat", "lon"),
        P("lat", "lon", None, None),
        P("lat", "lon", None, None, None),
        P("lat", "lon", None, None),
        P("lat", "lon", None, None),
    )
    out_specs = (P(None, "lat", "lon"), P("lat", "lon", None, None))
    return jax.shard_map(
        per_device, mesh=mesh, in_specs=in_specs, out_specs=out_specs, check_vma=False
    )
```

```python
import jax
import numpy as np
import jax.numpy as jnp
from jax import lax
from jax.experimental import pallas as pl
from jax.experimental.pallas import tpu as pltpu
from jax.sharding import PartitionSpec as P

LG = 8
LTOP = 4
FH = 8
FW = 16
K = 512
LANES = 128


def neighbours(edge_low, edge_high, axis):
    count = lax.axis_size(axis)
    forward = [(i, i + 1) for i in range(count - 1)]
    backward = [(target, source) for source, target in forward]
    return lax.ppermute(edge_high, axis, forward), lax.ppermute(edge_low, axis, backward)


def stencil(block):
    rows = block.shape[1]
    cols = block.shape[2]
    up, down = neighbours(block[:, 0:1, :], block[:, rows - 1 : rows, :], "lat")
    left, right = neighbours(block[:, :, 0], block[:, :, cols - 1], "lon")
    north = jnp.concatenate([up, lax.slice_in_dim(block, 0, rows - 1, axis=1)], 1)
    south = jnp.concatenate([lax.slice_in_dim(block, 1, rows, axis=1), down], 1)
    west = jnp.concatenate([left[:, :, None], lax.slice_in_dim(block, 0, cols - 1, axis=2)], 2)
    east = jnp.concatenate([lax.slice_in_dim(block, 1, cols, axis=2), right[:, :, None]], 2)
    return north + south + west + east - 4.0 * block


def columns(matrices, field, transpose):
    levels, height, breadth = field.shape
    blocks = matrices.shape[1]
    grouped = field.reshape(levels, height, blocks, breadth // blocks)
    form = "rbji,jrbc->irbc" if transpose else "rbij,jrbc->irbc"
    out = jnp.einsum(form, matrices, grouped, precision=lax.Precision.HIGHEST)
    return out.reshape(out.shape[0], height, breadth)


def window_gain(anchor_ref, gain_ref, s, tile_cols, tile_rows, sub, pad):
    span = FW + FH
    o = jnp.maximum(anchor_ref[s // 2, s % 2], 0)
    r = jnp.minimum(lax.div(o, tile_cols), tile_rows - FH)
    c = jnp.minimum(lax.rem(o, tile_cols), tile_cols - FW)
    c8 = pl.multiple_of(jnp.minimum(lax.div(c, FH) * FH, tile_cols - span), FH)
    off = c - c8
    g = jnp.concatenate([gain_ref[s], pad], axis=1)
    g = pltpu.roll(g, r * LTOP, 1)
    a = pltpu.roll(g[0:FH], lax.rem(off, FH), 0)
    b = pltpu.roll(g[FH:FW], lax.rem(off, FH), 0)
    low = sub >= off
    return c8, (jnp.where(low, a, 0.0), jnp.where(low, b, a), jnp.where(low, 0.0, b))


def predict_kernel(anchor_ref, obs_ref, top_ref, gain_ref, res_ref):
    tile_cols, wide = top_ref.shape
    slots, _, narrow = gain_ref.shape
    tile_rows = wide // LTOP
    span = FW + FH
    sub = lax.broadcasted_iota(jnp.int32, (FH, wide), 0)
    pad = jnp.zeros((FW, wide - narrow), jnp.float32)

    def predict(s, carry):
        c8, parts = window_gain(anchor_ref, gain_ref, s, tile_cols, tile_rows, sub, pad)
        win = top_ref[pl.ds(c8, span), :]
        acc = parts[0] * win[0:FH] + parts[1] * win[FH:FW] + parts[2] * win[FW:span]
        predicted = jnp.sum(acc, axis=(0, 1), keepdims=True)
        k = s // 2
        live = jnp.where(anchor_ref[k, s % 2] >= 0, 1.0, 0.0).astype(jnp.float32)
        res = (live * obs_ref[k, s % 2, 1]) * (predicted - obs_ref[k, s % 2, 0])
        res_ref[s] = jnp.broadcast_to(res, (1, LANES))
        return carry

    lax.fori_loop(0, slots, predict, 0, unroll=8)


def scatter_kernel(anchor_ref, res_ref, gain_ref, bar_ref):
    tile_cols, wide = bar_ref.shape
    slots, _, narrow = gain_ref.shape
    tile_rows = wide // LTOP
    span = FW + FH
    sub = lax.broadcasted_iota(jnp.int32, (FH, wide), 0)
    pad = jnp.zeros((FW, wide - narrow), jnp.float32)
    bar_ref[...] = jnp.zeros(bar_ref.shape, bar_ref.dtype)

    def scatter(s, carry):
        c8, parts = window_gain(anchor_ref, gain_ref, s, tile_cols, tile_rows, sub, pad)
        res = res_ref[s][0:1, 0:1]
        bar_ref[pl.ds(c8, span), :] += res * jnp.concatenate(parts, axis=0)
        return carry

    lax.fori_loop(0, slots, scatter, 0, unroll=8)


def predict(anchor, obs, top, gain):
    slots = gain.shape[0]
    smem = pl.BlockSpec(memory_space=pltpu.SMEM)
    vmem = pl.BlockSpec(memory_space=pltpu.VMEM)
    return pl.pallas_call(
        predict_kernel,
        out_shape=jax.ShapeDtypeStruct((slots, 1, LANES), jnp.float32),
        in_specs=[smem, smem, vmem, vmem],
        out_specs=vmem,
    )(anchor, obs, top, gain)


def scatter(anchor, res, gain, top_shape):
    smem = pl.BlockSpec(memory_space=pltpu.SMEM)
    vmem = pl.BlockSpec(memory_space=pltpu.VMEM)
    return pl.pallas_call(
        scatter_kernel,
        out_shape=jax.ShapeDtypeStruct(top_shape, jnp.float32),
        in_specs=[smem, vmem, vmem],
        out_specs=vmem,
    )(anchor, res, gain)


def reorder_matrix():
    source = np.arange(K)
    layer_of = source // (FH * FW)
    row_of = (source // FW) % FH
    col_of = source % FW
    matrix = np.zeros((K, K), np.float32)
    matrix[source, (col_of * FH + row_of) * LTOP + layer_of] = 1.0
    return matrix


def per_device(
    moisture,
    conductance,
    inverse,
    crop_mask,
    adjoint_in,
    foot_anchor,
    antenna_gain,
    obs_value,
    obs_weight,
):
    levels, tile_rows, tile_cols = moisture.shape
    mask_float = crop_mask.astype(jnp.float32)
    blocks = inverse.shape[1]
    matrices = inverse.reshape(tile_rows, blocks, levels, levels)

    owner_gain = antenna_gain[0, 0]
    owners, slots_per, _ = owner_gain.shape
    packed = jnp.concatenate(
        [owner_gain, obs_value[0, 0][..., None], obs_weight[0, 0][..., None]], -1
    )
    received = lax.all_to_all(packed, "lon", split_axis=0, concat_axis=0, tiled=True)
    slots = owners * slots_per
    gain = jnp.dot(
        received[..., :K].reshape(slots, K), jnp.asarray(reorder_matrix()), precision=lax.Precision.HIGHEST
    )
    gain = gain.reshape(slots, FW, FH * LTOP)
    obs = received[..., K : K + 2]

    deep = moisture[levels - LG :]
    mixed = jnp.concatenate(
        [moisture[: levels - LG], deep + conductance * stencil(deep)], 0
    )
    solved_top = columns(matrices[:, :, :LTOP, :], mixed, False)
    topmost = (solved_top * mask_float).transpose(2, 1, 0).reshape(tile_cols, tile_rows * LTOP)

    slot_anchor = foot_anchor[0, 0]
    res_rows = predict(slot_anchor, obs, topmost, gain)
    residual_out = lax.all_to_all(
        res_rows[:, 0, 0].reshape(owners, slots_per), "lon", split_axis=0, concat_axis=0, tiled=True
    )
    bar = scatter(slot_anchor, res_rows, gain, topmost.shape)
    bar, residual_out = lax.optimization_barrier((bar, residual_out))

    base = columns(matrices, adjoint_in, True)
    topbar = bar.reshape(tile_cols, tile_rows, LTOP).transpose(2, 1, 0) * mask_float
    mixedbar = base + columns(matrices[:, :, :LTOP, :], topbar, True)
    deepbar = mixedbar[levels - LG :]
    gradient = jnp.concatenate(
        [mixedbar[: levels - LG], deepbar + stencil(conductance * deepbar)], 0
    )
    return gradient, residual_out[None, None]


def solution(mesh):
    in_specs = (
        P(None, "lat", "lon"),
        P("lat", "lon"),
        P("lat", "lon", None),
        P("lat", "lon"),
        P(None, "lat", "lon"),
        P("lat", "lon", None, None),
        P("lat", "lon", None, None, None),
        P("lat", "lon", None, None),
        P("lat", "lon", None, None),
    )
    out_specs = (P(None, "lat", "lon"), P("lat", "lon", None, None))
    return jax.shard_map(
        per_device, mesh=mesh, in_specs=in_specs, out_specs=out_specs, check_vma=False
    )
```

```python
import jax
import numpy as np
import jax.numpy as jnp
from jax import lax
from jax.experimental import pallas as pl
from jax.experimental.pallas import tpu as pltpu
from jax.sharding import PartitionSpec as P

LG = 8
LTOP = 4
FH = 8
FW = 16
K = 512
LANES = 128


def neighbours(edge_low, edge_high, axis):
    count = lax.axis_size(axis)
    forward = [(i, i + 1) for i in range(count - 1)]
    backward = [(target, source) for source, target in forward]
    return lax.ppermute(edge_high, axis, forward), lax.ppermute(edge_low, axis, backward)


def stencil(block):
    rows = block.shape[1]
    cols = block.shape[2]
    up, down = neighbours(block[:, 0:1, :], block[:, rows - 1 : rows, :], "lat")
    left, right = neighbours(block[:, :, 0], block[:, :, cols - 1], "lon")
    north = jnp.concatenate([up, lax.slice_in_dim(block, 0, rows - 1, axis=1)], 1)
    south = jnp.concatenate([lax.slice_in_dim(block, 1, rows, axis=1), down], 1)
    west = jnp.concatenate([left[:, :, None], lax.slice_in_dim(block, 0, cols - 1, axis=2)], 2)
    east = jnp.concatenate([lax.slice_in_dim(block, 1, cols, axis=2), right[:, :, None]], 2)
    return north + south + west + east - 4.0 * block


def columns(matrices, field, transpose):
    levels, height, breadth = field.shape
    blocks = matrices.shape[1]
    grouped = field.reshape(levels, height, blocks, breadth // blocks)
    form = "rbji,jrbc->irbc" if transpose else "rbij,jrbc->irbc"
    out = jnp.einsum(form, matrices, grouped, precision=lax.Precision.HIGHEST)
    return out.reshape(out.shape[0], height, breadth)


def window_gain(anchor_ref, gain_ref, s, tile_cols, tile_rows, sub, pad):
    span = FW + FH
    o = jnp.maximum(anchor_ref[s // 2, s % 2], 0)
    r = jnp.minimum(lax.div(o, tile_cols), tile_rows - FH)
    c = jnp.minimum(lax.rem(o, tile_cols), tile_cols - FW)
    c8 = pl.multiple_of(jnp.minimum(lax.div(c, FH) * FH, tile_cols - span), FH)
    off = c - c8
    g = jnp.concatenate([gain_ref[s], pad], axis=1)
    g = pltpu.roll(g, r * LTOP, 1)
    a = pltpu.roll(g[0:FH], lax.rem(off, FH), 0)
    b = pltpu.roll(g[FH:FW], lax.rem(off, FH), 0)
    low = sub >= off
    return c8, (jnp.where(low, a, 0.0), jnp.where(low, b, a), jnp.where(low, 0.0, b))


def predict_kernel(anchor_ref, top_ref, gain_ref, part_ref):
    tile_cols, wide = top_ref.shape
    slots, _, narrow = gain_ref.shape
    tile_rows = wide // LTOP
    span = FW + FH
    sub = lax.broadcasted_iota(jnp.int32, (FH, wide), 0)
    pad = jnp.zeros((FW, wide - narrow), jnp.float32)

    def predict(s, carry):
        c8, parts = window_gain(anchor_ref, gain_ref, s, tile_cols, tile_rows, sub, pad)
        win = top_ref[pl.ds(c8, span), :]
        part_ref[s] = parts[0] * win[0:FH] + parts[1] * win[FH:FW] + parts[2] * win[FW:span]
        return carry

    lax.fori_loop(0, slots, predict, 0, unroll=8)


def scatter_kernel(anchor_ref, res_ref, gain_ref, bar_ref):
    tile_cols, wide = bar_ref.shape
    slots, _, narrow = gain_ref.shape
    tile_rows = wide // LTOP
    span = FW + FH
    sub = lax.broadcasted_iota(jnp.int32, (FH, wide), 0)
    pad = jnp.zeros((FW, wide - narrow), jnp.float32)
    bar_ref[...] = jnp.zeros(bar_ref.shape, bar_ref.dtype)

    def scatter(s, carry):
        c8, parts = window_gain(anchor_ref, gain_ref, s, tile_cols, tile_rows, sub, pad)
        bar_ref[pl.ds(c8, span), :] += res_ref[s] * jnp.concatenate(parts, axis=0)
        return carry

    lax.fori_loop(0, slots, scatter, 0, unroll=8)


def predict(anchor, top, gain):
    slots = gain.shape[0]
    smem = pl.BlockSpec(memory_space=pltpu.SMEM)
    vmem = pl.BlockSpec(memory_space=pltpu.VMEM)
    return pl.pallas_call(
        predict_kernel,
        out_shape=jax.ShapeDtypeStruct((slots, FH, top.shape[1]), jnp.float32),
        in_specs=[smem, vmem, vmem],
        out_specs=vmem,
    )(anchor, top, gain)


def scatter(anchor, res, gain, top_shape):
    smem = pl.BlockSpec(memory_space=pltpu.SMEM)
    vmem = pl.BlockSpec(memory_space=pltpu.VMEM)
    return pl.pallas_call(
        scatter_kernel,
        out_shape=jax.ShapeDtypeStruct(top_shape, jnp.float32),
        in_specs=[smem, smem, vmem],
        out_specs=vmem,
    )(anchor, res, gain)


def reorder_matrix():
    source = np.arange(K)
    layer_of = source // (FH * FW)
    row_of = (source // FW) % FH
    col_of = source % FW
    matrix = np.zeros((K, K), np.float32)
    matrix[source, (col_of * FH + row_of) * LTOP + layer_of] = 1.0
    return matrix


def per_device(
    moisture,
    conductance,
    inverse,
    crop_mask,
    adjoint_in,
    foot_anchor,
    antenna_gain,
    obs_value,
    obs_weight,
):
    levels, tile_rows, tile_cols = moisture.shape
    mask_float = crop_mask.astype(jnp.float32)
    blocks = inverse.shape[1]
    matrices = inverse.reshape(tile_rows, blocks, levels, levels)

    owner_gain = antenna_gain[0, 0]
    owners, slots_per, _ = owner_gain.shape
    packed = jnp.concatenate(
        [owner_gain, obs_value[0, 0][..., None], obs_weight[0, 0][..., None]], -1
    )
    received = lax.all_to_all(packed, "lon", split_axis=0, concat_axis=0, tiled=True)
    slots = owners * slots_per
    gain = jnp.dot(
        received[..., :K].reshape(slots, K), jnp.asarray(reorder_matrix()), precision=lax.Precision.HIGHEST
    )
    gain = gain.reshape(slots, FW, FH * LTOP)
    value = received[..., K]
    weight = received[..., K + 1]

    deep = moisture[levels - LG :]
    mixed = jnp.concatenate(
        [moisture[: levels - LG], deep + conductance * stencil(deep)], 0
    )
    solved_top = columns(matrices[:, :, :LTOP, :], mixed, False)
    topmost = (solved_top * mask_float).transpose(2, 1, 0).reshape(tile_cols, tile_rows * LTOP)

    slot_anchor = foot_anchor[0, 0]
    parts = predict(slot_anchor, topmost, gain)
    predicted = jnp.sum(parts, axis=(1, 2)).reshape(owners, slots_per)
    live = (slot_anchor >= 0).astype(jnp.float32)
    residual = live * weight * (predicted - value)
    residual_out = lax.all_to_all(residual, "lon", split_axis=0, concat_axis=0, tiled=True)
    bar = scatter(slot_anchor, residual.reshape(slots), gain, topmost.shape)
    bar, residual_out = lax.optimization_barrier((bar, residual_out))

    base = columns(matrices, adjoint_in, True)
    topbar = bar.reshape(tile_cols, tile_rows, LTOP).transpose(2, 1, 0) * mask_float
    mixedbar = base + columns(matrices[:, :, :LTOP, :], topbar, True)
    deepbar = mixedbar[levels - LG :]
    gradient = jnp.concatenate(
        [mixedbar[: levels - LG], deepbar + stencil(conductance * deepbar)], 0
    )
    return gradient, residual_out[None, None]


def solution(mesh):
    in_specs = (
        P(None, "lat", "lon"),
        P("lat", "lon"),
        P("lat", "lon", None),
        P("lat", "lon"),
        P(None, "lat", "lon"),
        P("lat", "lon", None, None),
        P("lat", "lon", None, None, None),
        P("lat", "lon", None, None),
        P("lat", "lon", None, None),
    )
    out_specs = (P(None, "lat", "lon"), P("lat", "lon", None, None))
    return jax.shard_map(
        per_device, mesh=mesh, in_specs=in_specs, out_specs=out_specs, check_vma=False
    )
```

```python
import jax
import numpy as np
import jax.numpy as jnp
from jax import lax
from jax.experimental import pallas as pl
from jax.experimental.pallas import tpu as pltpu
from jax.sharding import PartitionSpec as P

LG = 8
LTOP = 4
FH = 8
FW = 16
K = 512
LANES = 128


def neighbours(edge_low, edge_high, axis):
    count = lax.axis_size(axis)
    forward = [(i, i + 1) for i in range(count - 1)]
    backward = [(target, source) for source, target in forward]
    return lax.ppermute(edge_high, axis, forward), lax.ppermute(edge_low, axis, backward)


def stencil(block):
    rows = block.shape[1]
    cols = block.shape[2]
    up, down = neighbours(block[:, 0:1, :], block[:, rows - 1 : rows, :], "lat")
    left, right = neighbours(block[:, :, 0], block[:, :, cols - 1], "lon")
    north = jnp.concatenate([up, lax.slice_in_dim(block, 0, rows - 1, axis=1)], 1)
    south = jnp.concatenate([lax.slice_in_dim(block, 1, rows, axis=1), down], 1)
    west = jnp.concatenate([left[:, :, None], lax.slice_in_dim(block, 0, cols - 1, axis=2)], 2)
    east = jnp.concatenate([lax.slice_in_dim(block, 1, cols, axis=2), right[:, :, None]], 2)
    return north + south + west + east - 4.0 * block


def columns(matrices, field, transpose):
    levels, height, breadth = field.shape
    blocks = matrices.shape[1]
    grouped = field.reshape(levels, height, blocks, breadth // blocks)
    form = "rbji,jrbc->irbc" if transpose else "rbij,jrbc->irbc"
    out = jnp.einsum(form, matrices, grouped, precision=lax.Precision.HIGHEST)
    return out.reshape(out.shape[0], height, breadth)


def window_gain(anchor_ref, gain_ref, s, tile_cols, tile_rows, sub, pad):
    span = FW + FH
    o = jnp.maximum(anchor_ref[s // 2, s % 2], 0)
    r = jnp.minimum(lax.div(o, tile_cols), tile_rows - FH)
    c = jnp.minimum(lax.rem(o, tile_cols), tile_cols - FW)
    c8 = pl.multiple_of(jnp.minimum(lax.div(c, FH) * FH, tile_cols - span), FH)
    off = c - c8
    g = jnp.concatenate([gain_ref[s], pad], axis=1)
    g = pltpu.roll(g, r * LTOP, 1)
    a = pltpu.roll(g[0:FH], lax.rem(off, FH), 0)
    b = pltpu.roll(g[FH:FW], lax.rem(off, FH), 0)
    low = sub >= off
    return c8, (jnp.where(low, a, 0.0), jnp.where(low, b, a), jnp.where(low, 0.0, b))


def predict_kernel(anchor_ref, top_ref, gain_ref, part_ref):
    tile_cols, wide = top_ref.shape
    slots, _, narrow = gain_ref.shape
    tile_rows = wide // LTOP
    span = FW + FH
    sub = lax.broadcasted_iota(jnp.int32, (FH, wide), 0)
    pad = jnp.zeros((FW, wide - narrow), jnp.float32)

    def predict(s, carry):
        c8, parts = window_gain(anchor_ref, gain_ref, s, tile_cols, tile_rows, sub, pad)
        win = top_ref[pl.ds(c8, span), :]
        part_ref[s] = parts[0] * win[0:FH] + parts[1] * win[FH:FW] + parts[2] * win[FW:span]
        return carry

    lax.fori_loop(0, slots, predict, 0, unroll=8)


def scatter_kernel(anchor_ref, res_ref, gain_ref, bar_ref):
    tile_cols, wide = bar_ref.shape
    slots, _, narrow = gain_ref.shape
    tile_rows = wide // LTOP
    span = FW + FH
    sub = lax.broadcasted_iota(jnp.int32, (FH, wide), 0)
    pad = jnp.zeros((FW, wide - narrow), jnp.float32)
    bar_ref[...] = jnp.zeros(bar_ref.shape, bar_ref.dtype)

    def scatter(s, carry):
        c8, parts = window_gain(anchor_ref, gain_ref, s, tile_cols, tile_rows, sub, pad)
        bar_ref[pl.ds(c8, span), :] += res_ref[s] * jnp.concatenate(parts, axis=0)
        return carry

    lax.fori_loop(0, slots, scatter, 0, unroll=8)


def predict(anchor, top, gain):
    slots = gain.shape[0]
    smem = pl.BlockSpec(memory_space=pltpu.SMEM)
    vmem = pl.BlockSpec(memory_space=pltpu.VMEM)
    return pl.pallas_call(
        predict_kernel,
        out_shape=jax.ShapeDtypeStruct((slots, FH, top.shape[1]), jnp.float32),
        in_specs=[smem, vmem, vmem],
        out_specs=vmem,
    )(anchor, top, gain)


def scatter(anchor, res, gain, top_shape):
    smem = pl.BlockSpec(memory_space=pltpu.SMEM)
    vmem = pl.BlockSpec(memory_space=pltpu.VMEM)
    return pl.pallas_call(
        scatter_kernel,
        out_shape=jax.ShapeDtypeStruct(top_shape, jnp.float32),
        in_specs=[smem, smem, vmem],
        out_specs=vmem,
    )(anchor, res, gain)


def reorder_matrix():
    source = np.arange(K)
    layer_of = source // (FH * FW)
    row_of = (source // FW) % FH
    col_of = source % FW
    matrix = np.zeros((K, K), np.float32)
    matrix[source, (col_of * FH + row_of) * LTOP + layer_of] = 1.0
    return matrix


def per_device(
    moisture,
    conductance,
    inverse,
    crop_mask,
    adjoint_in,
    foot_anchor,
    antenna_gain,
    obs_value,
    obs_weight,
):
    levels, tile_rows, tile_cols = moisture.shape
    mask_float = crop_mask.astype(jnp.float32)
    blocks = inverse.shape[1]
    matrices = inverse.reshape(tile_rows, blocks, levels, levels)

    owner_gain = antenna_gain[0, 0]
    owners, slots_per, _ = owner_gain.shape
    packed = jnp.pad(owner_gain, ((0, 0), (0, 0), (0, 2)))
    packed = packed.at[:, :, K].set(obs_value[0, 0]).at[:, :, K + 1].set(obs_weight[0, 0])
    received = lax.all_to_all(packed, "lon", split_axis=0, concat_axis=0, tiled=True)
    slots = owners * slots_per
    gain = jnp.dot(
        received[..., :K].reshape(slots, K), jnp.asarray(reorder_matrix()), precision=lax.Precision.HIGHEST
    )
    gain = gain.reshape(slots, FW, FH * LTOP)
    value = received[..., K]
    weight = received[..., K + 1]

    deep = moisture[levels - LG :]
    mixed = jnp.concatenate(
        [moisture[: levels - LG], deep + conductance * stencil(deep)], 0
    )
    solved_top = columns(matrices[:, :, :LTOP, :], mixed, False)
    topmost = (solved_top * mask_float).transpose(2, 1, 0).reshape(tile_cols, tile_rows * LTOP)

    slot_anchor = foot_anchor[0, 0]
    parts = predict(slot_anchor, topmost, gain)
    predicted = jnp.sum(parts, axis=(1, 2)).reshape(owners, slots_per)
    live = (slot_anchor >= 0).astype(jnp.float32)
    residual = live * weight * (predicted - value)
    residual_out = lax.all_to_all(residual, "lon", split_axis=0, concat_axis=0, tiled=True)
    bar = scatter(slot_anchor, residual.reshape(slots), gain, topmost.shape)
    bar, residual_out = lax.optimization_barrier((bar, residual_out))

    base = columns(matrices, adjoint_in, True)
    topbar = bar.reshape(tile_cols, tile_rows, LTOP).transpose(2, 1, 0) * mask_float
    mixedbar = base + columns(matrices[:, :, :LTOP, :], topbar, True)
    deepbar = mixedbar[levels - LG :]
    gradient = jnp.concatenate(
        [mixedbar[: levels - LG], deepbar + stencil(conductance * deepbar)], 0
    )
    return gradient, residual_out[None, None]


def solution(mesh):
    in_specs = (
        P(None, "lat", "lon"),
        P("lat", "lon"),
        P("lat", "lon", None),
        P("lat", "lon"),
        P(None, "lat", "lon"),
        P("lat", "lon", None, None),
        P("lat", "lon", None, None, None),
        P("lat", "lon", None, None),
        P("lat", "lon", None, None),
    )
    out_specs = (P(None, "lat", "lon"), P("lat", "lon", None, None))
    return jax.shard_map(
        per_device, mesh=mesh, in_specs=in_specs, out_specs=out_specs, check_vma=False
    )
```

```python
import jax
import numpy as np
import jax.numpy as jnp
from jax import lax
from jax.experimental import pallas as pl
from jax.experimental.pallas import tpu as pltpu
from jax.sharding import PartitionSpec as P

LG = 8
LTOP = 4
FH = 8
FW = 16
K = 512
LANES = 128


def neighbours(edge_low, edge_high, axis):
    count = lax.axis_size(axis)
    forward = [(i, i + 1) for i in range(count - 1)]
    backward = [(target, source) for source, target in forward]
    return lax.ppermute(edge_high, axis, forward), lax.ppermute(edge_low, axis, backward)


def stencil(block):
    rows = block.shape[1]
    cols = block.shape[2]
    up, down = neighbours(block[:, 0:1, :], block[:, rows - 1 : rows, :], "lat")
    left, right = neighbours(block[:, :, 0], block[:, :, cols - 1], "lon")
    north = jnp.concatenate([up, lax.slice_in_dim(block, 0, rows - 1, axis=1)], 1)
    south = jnp.concatenate([lax.slice_in_dim(block, 1, rows, axis=1), down], 1)
    west = jnp.concatenate([left[:, :, None], lax.slice_in_dim(block, 0, cols - 1, axis=2)], 2)
    east = jnp.concatenate([lax.slice_in_dim(block, 1, cols, axis=2), right[:, :, None]], 2)
    return north + south + west + east - 4.0 * block


def columns(matrices, field, transpose):
    levels, height, breadth = field.shape
    blocks = matrices.shape[1]
    grouped = field.reshape(levels, height, blocks, breadth // blocks)
    form = "rbji,jrbc->irbc" if transpose else "rbij,jrbc->irbc"
    out = jnp.einsum(form, matrices, grouped, precision=lax.Precision.HIGHEST)
    return out.reshape(out.shape[0], height, breadth)


def window_gain(anchor_ref, gain_ref, s, tile_cols, tile_rows, sub, pad):
    span = FW + FH
    o = jnp.maximum(anchor_ref[s // 2, s % 2], 0)
    r = jnp.minimum(lax.div(o, tile_cols), tile_rows - FH)
    c = jnp.minimum(lax.rem(o, tile_cols), tile_cols - FW)
    c8 = pl.multiple_of(jnp.minimum(lax.div(c, FH) * FH, tile_cols - span), FH)
    off = c - c8
    g = jnp.concatenate([gain_ref[s], pad], axis=1)
    g = pltpu.roll(g, r * LTOP, 1)
    a = pltpu.roll(g[0:FH], lax.rem(off, FH), 0)
    b = pltpu.roll(g[FH:FW], lax.rem(off, FH), 0)
    low = sub >= off
    return c8, (jnp.where(low, a, 0.0), jnp.where(low, b, a), jnp.where(low, 0.0, b))


def predict_kernel(anchor_ref, top_ref, gain_ref, part_ref):
    tile_cols, wide = top_ref.shape
    slots, _, narrow = gain_ref.shape
    tile_rows = wide // LTOP
    span = FW + FH
    sub = lax.broadcasted_iota(jnp.int32, (FH, wide), 0)
    pad = jnp.zeros((FW, wide - narrow), jnp.float32)

    def predict(s, carry):
        c8, parts = window_gain(anchor_ref, gain_ref, s, tile_cols, tile_rows, sub, pad)
        win = top_ref[pl.ds(c8, span), :]
        part_ref[s] = parts[0] * win[0:FH] + parts[1] * win[FH:FW] + parts[2] * win[FW:span]
        return carry

    lax.fori_loop(0, slots, predict, 0, unroll=8)


def scatter_kernel(anchor_ref, res_ref, gain_ref, bar_ref):
    tile_cols, wide = bar_ref.shape
    slots, _, narrow = gain_ref.shape
    tile_rows = wide // LTOP
    span = FW + FH
    sub = lax.broadcasted_iota(jnp.int32, (FH, wide), 0)
    pad = jnp.zeros((FW, wide - narrow), jnp.float32)
    bar_ref[...] = jnp.zeros(bar_ref.shape, bar_ref.dtype)

    def scatter(s, carry):
        c8, parts = window_gain(anchor_ref, gain_ref, s, tile_cols, tile_rows, sub, pad)
        bar_ref[pl.ds(c8, span), :] += res_ref[s] * jnp.concatenate(parts, axis=0)
        return carry

    lax.fori_loop(0, slots, scatter, 0, unroll=8)


def predict(anchor, top, gain):
    slots = gain.shape[0]
    smem = pl.BlockSpec(memory_space=pltpu.SMEM)
    vmem = pl.BlockSpec(memory_space=pltpu.VMEM)
    return pl.pallas_call(
        predict_kernel,
        out_shape=jax.ShapeDtypeStruct((slots, FH, top.shape[1]), jnp.float32),
        in_specs=[smem, vmem, vmem],
        out_specs=vmem,
    )(anchor, top, gain)


def scatter(anchor, res, gain, top_shape):
    smem = pl.BlockSpec(memory_space=pltpu.SMEM)
    vmem = pl.BlockSpec(memory_space=pltpu.VMEM)
    return pl.pallas_call(
        scatter_kernel,
        out_shape=jax.ShapeDtypeStruct(top_shape, jnp.float32),
        in_specs=[smem, smem, vmem],
        out_specs=vmem,
    )(anchor, res, gain)


def reorder_matrix():
    source = np.arange(K)
    layer_of = source // (FH * FW)
    row_of = (source // FW) % FH
    col_of = source % FW
    matrix = np.zeros((K, K), np.float32)
    matrix[source, (col_of * FH + row_of) * LTOP + layer_of] = 1.0
    return matrix


def per_device(
    moisture,
    conductance,
    inverse,
    crop_mask,
    adjoint_in,
    foot_anchor,
    antenna_gain,
    obs_value,
    obs_weight,
):
    levels, tile_rows, tile_cols = moisture.shape
    mask_float = crop_mask.astype(jnp.float32)
    blocks = inverse.shape[1]
    matrices = inverse.reshape(tile_rows, blocks, levels, levels)

    owner_gain = antenna_gain[0, 0]
    owners, slots_per, _ = owner_gain.shape
    packed = jnp.concatenate(
        [owner_gain.reshape(owners, slots_per * K), obs_value[0, 0], obs_weight[0, 0]], -1
    )
    received = lax.all_to_all(packed, "lon", split_axis=0, concat_axis=0, tiled=True)
    slots = owners * slots_per
    gain = jnp.dot(
        received[:, : slots_per * K].reshape(slots, K), jnp.asarray(reorder_matrix()), precision=lax.Precision.HIGHEST
    )
    gain = gain.reshape(slots, FW, FH * LTOP)
    value = received[:, slots_per * K : slots_per * (K + 1)]
    weight = received[:, slots_per * (K + 1) :]

    deep = moisture[levels - LG :]
    mixed = jnp.concatenate(
        [moisture[: levels - LG], deep + conductance * stencil(deep)], 0
    )
    solved_top = columns(matrices[:, :, :LTOP, :], mixed, False)
    topmost = (solved_top * mask_float).transpose(2, 1, 0).reshape(tile_cols, tile_rows * LTOP)

    slot_anchor = foot_anchor[0, 0]
    parts = predict(slot_anchor, topmost, gain)
    predicted = jnp.sum(parts, axis=(1, 2)).reshape(owners, slots_per)
    live = (slot_anchor >= 0).astype(jnp.float32)
    residual = live * weight * (predicted - value)
    residual_out = lax.all_to_all(residual, "lon", split_axis=0, concat_axis=0, tiled=True)
    bar = scatter(slot_anchor, residual.reshape(slots), gain, topmost.shape)
    bar, residual_out = lax.optimization_barrier((bar, residual_out))

    base = columns(matrices, adjoint_in, True)
    topbar = bar.reshape(tile_cols, tile_rows, LTOP).transpose(2, 1, 0) * mask_float
    mixedbar = base + columns(matrices[:, :, :LTOP, :], topbar, True)
    deepbar = mixedbar[levels - LG :]
    gradient = jnp.concatenate(
        [mixedbar[: levels - LG], deepbar + stencil(conductance * deepbar)], 0
    )
    return gradient, residual_out[None, None]


def solution(mesh):
    in_specs = (
        P(None, "lat", "lon"),
        P("lat", "lon"),
        P("lat", "lon", None),
        P("lat", "lon"),
        P(None, "lat", "lon"),
        P("lat", "lon", None, None),
        P("lat", "lon", None, None, None),
        P("lat", "lon", None, None),
        P("lat", "lon", None, None),
    )
    out_specs = (P(None, "lat", "lon"), P("lat", "lon", None, None))
    return jax.shard_map(
        per_device, mesh=mesh, in_specs=in_specs, out_specs=out_specs, check_vma=False
    )
```

```python
import jax
import numpy as np
import jax.numpy as jnp
from jax import lax
from jax.experimental import pallas as pl
from jax.experimental.pallas import tpu as pltpu
from jax.sharding import PartitionSpec as P

LG = 8
LTOP = 4
FH = 8
FW = 16
K = 512
LANES = 128


def neighbours(edge_low, edge_high, axis):
    count = lax.axis_size(axis)
    forward = [(i, i + 1) for i in range(count - 1)]
    backward = [(target, source) for source, target in forward]
    return lax.ppermute(edge_high, axis, forward), lax.ppermute(edge_low, axis, backward)


def stencil(block):
    rows = block.shape[1]
    cols = block.shape[2]
    up, down = neighbours(block[:, 0:1, :], block[:, rows - 1 : rows, :], "lat")
    left, right = neighbours(block[:, :, 0], block[:, :, cols - 1], "lon")
    north = jnp.concatenate([up, lax.slice_in_dim(block, 0, rows - 1, axis=1)], 1)
    south = jnp.concatenate([lax.slice_in_dim(block, 1, rows, axis=1), down], 1)
    west = jnp.concatenate([left[:, :, None], lax.slice_in_dim(block, 0, cols - 1, axis=2)], 2)
    east = jnp.concatenate([lax.slice_in_dim(block, 1, cols, axis=2), right[:, :, None]], 2)
    return north + south + west + east - 4.0 * block


def columns(matrices, field, transpose):
    levels, height, breadth = field.shape
    blocks = matrices.shape[1]
    grouped = field.reshape(levels, height, blocks, breadth // blocks)
    form = "rbji,jrbc->irbc" if transpose else "rbij,jrbc->irbc"
    out = jnp.einsum(form, matrices, grouped, precision=lax.Precision.HIGHEST)
    return out.reshape(out.shape[0], height, breadth)


def window_gain(anchor_ref, gain_ref, s, tile_cols, tile_rows, sub, pad):
    span = FW + FH
    o = jnp.maximum(anchor_ref[s // 2, s % 2], 0)
    r = jnp.minimum(lax.div(o, tile_cols), tile_rows - FH)
    c = jnp.minimum(lax.rem(o, tile_cols), tile_cols - FW)
    c8 = pl.multiple_of(jnp.minimum(lax.div(c, FH) * FH, tile_cols - span), FH)
    off = c - c8
    g = jnp.concatenate([gain_ref[s], pad], axis=1)
    g = pltpu.roll(g, r * LTOP, 1)
    a = pltpu.roll(g[0:FH], lax.rem(off, FH), 0)
    b = pltpu.roll(g[FH:FW], lax.rem(off, FH), 0)
    low = sub >= off
    return c8, (jnp.where(low, a, 0.0), jnp.where(low, b, a), jnp.where(low, 0.0, b))


def predict_kernel(anchor_ref, top_ref, gain_ref, part_ref):
    tile_cols, wide = top_ref.shape
    slots, _, narrow = gain_ref.shape
    tile_rows = wide // LTOP
    span = FW + FH
    sub = lax.broadcasted_iota(jnp.int32, (FH, wide), 0)
    pad = jnp.zeros((FW, wide - narrow), jnp.float32)

    def predict(s, carry):
        c8, parts = window_gain(anchor_ref, gain_ref, s, tile_cols, tile_rows, sub, pad)
        win = top_ref[pl.ds(c8, span), :]
        part_ref[s] = parts[0] * win[0:FH] + parts[1] * win[FH:FW] + parts[2] * win[FW:span]
        return carry

    lax.fori_loop(0, slots, predict, 0, unroll=16)


def scatter_kernel(anchor_ref, res_ref, gain_ref, bar_ref):
    tile_cols, wide = bar_ref.shape
    slots, _, narrow = gain_ref.shape
    tile_rows = wide // LTOP
    span = FW + FH
    sub = lax.broadcasted_iota(jnp.int32, (FH, wide), 0)
    pad = jnp.zeros((FW, wide - narrow), jnp.float32)
    bar_ref[...] = jnp.zeros(bar_ref.shape, bar_ref.dtype)

    def scatter(s, carry):
        c8, parts = window_gain(anchor_ref, gain_ref, s, tile_cols, tile_rows, sub, pad)
        bar_ref[pl.ds(c8, span), :] += res_ref[s] * jnp.concatenate(parts, axis=0)
        return carry

    lax.fori_loop(0, slots, scatter, 0, unroll=16)


def predict(anchor, top, gain):
    slots = gain.shape[0]
    smem = pl.BlockSpec(memory_space=pltpu.SMEM)
    vmem = pl.BlockSpec(memory_space=pltpu.VMEM)
    return pl.pallas_call(
        predict_kernel,
        out_shape=jax.ShapeDtypeStruct((slots, FH, top.shape[1]), jnp.float32),
        in_specs=[smem, vmem, vmem],
        out_specs=vmem,
    )(anchor, top, gain)


def scatter(anchor, res, gain, top_shape):
    smem = pl.BlockSpec(memory_space=pltpu.SMEM)
    vmem = pl.BlockSpec(memory_space=pltpu.VMEM)
    return pl.pallas_call(
        scatter_kernel,
        out_shape=jax.ShapeDtypeStruct(top_shape, jnp.float32),
        in_specs=[smem, smem, vmem],
        out_specs=vmem,
    )(anchor, res, gain)


def reorder_matrix():
    source = np.arange(K)
    layer_of = source // (FH * FW)
    row_of = (source // FW) % FH
    col_of = source % FW
    matrix = np.zeros((K, K), np.float32)
    matrix[source, (col_of * FH + row_of) * LTOP + layer_of] = 1.0
    return matrix


def per_device(
    moisture,
    conductance,
    inverse,
    crop_mask,
    adjoint_in,
    foot_anchor,
    antenna_gain,
    obs_value,
    obs_weight,
):
    levels, tile_rows, tile_cols = moisture.shape
    mask_float = crop_mask.astype(jnp.float32)
    blocks = inverse.shape[1]
    matrices = inverse.reshape(tile_rows, blocks, levels, levels)

    owner_gain = antenna_gain[0, 0]
    owners, slots_per, _ = owner_gain.shape
    packed = jnp.concatenate(
        [owner_gain.reshape(owners, slots_per * K), obs_value[0, 0], obs_weight[0, 0]], -1
    )
    received = lax.all_to_all(packed, "lon", split_axis=0, concat_axis=0, tiled=True)
    slots = owners * slots_per
    gain = jnp.dot(
        received[:, : slots_per * K].reshape(slots, K), jnp.asarray(reorder_matrix()), precision=lax.Precision.HIGHEST
    )
    gain = gain.reshape(slots, FW, FH * LTOP)
    value = received[:, slots_per * K : slots_per * (K + 1)]
    weight = received[:, slots_per * (K + 1) :]

    deep = moisture[levels - LG :]
    mixed = jnp.concatenate(
        [moisture[: levels - LG], deep + conductance * stencil(deep)], 0
    )
    solved_top = columns(matrices[:, :, :LTOP, :], mixed, False)
    topmost = (solved_top * mask_float).transpose(2, 1, 0).reshape(tile_cols, tile_rows * LTOP)

    slot_anchor = foot_anchor[0, 0]
    parts = predict(slot_anchor, topmost, gain)
    predicted = jnp.sum(parts, axis=(1, 2)).reshape(owners, slots_per)
    live = (slot_anchor >= 0).astype(jnp.float32)
    residual = live * weight * (predicted - value)
    residual_out = lax.all_to_all(residual, "lon", split_axis=0, concat_axis=0, tiled=True)
    bar = scatter(slot_anchor, residual.reshape(slots), gain, topmost.shape)
    bar, residual_out = lax.optimization_barrier((bar, residual_out))

    base = columns(matrices, adjoint_in, True)
    topbar = bar.reshape(tile_cols, tile_rows, LTOP).transpose(2, 1, 0) * mask_float
    mixedbar = base + columns(matrices[:, :, :LTOP, :], topbar, True)
    deepbar = mixedbar[levels - LG :]
    gradient = jnp.concatenate(
        [mixedbar[: levels - LG], deepbar + stencil(conductance * deepbar)], 0
    )
    return gradient, residual_out[None, None]


def solution(mesh):
    in_specs = (
        P(None, "lat", "lon"),
        P("lat", "lon"),
        P("lat", "lon", None),
        P("lat", "lon"),
        P(None, "lat", "lon"),
        P("lat", "lon", None, None),
        P("lat", "lon", None, None, None),
        P("lat", "lon", None, None),
        P("lat", "lon", None, None),
    )
    out_specs = (P(None, "lat", "lon"), P("lat", "lon", None, None))
    return jax.shard_map(
        per_device, mesh=mesh, in_specs=in_specs, out_specs=out_specs, check_vma=False
    )
```

```python
import jax
import numpy as np
import jax.numpy as jnp
from jax import lax
from jax.experimental import pallas as pl
from jax.experimental.pallas import tpu as pltpu
from jax.sharding import PartitionSpec as P

LG = 8
LTOP = 4
FH = 8
FW = 16
K = 512
LANES = 128


def neighbours(edge_low, edge_high, axis):
    count = lax.axis_size(axis)
    forward = [(i, i + 1) for i in range(count - 1)]
    backward = [(target, source) for source, target in forward]
    return lax.ppermute(edge_high, axis, forward), lax.ppermute(edge_low, axis, backward)


def stencil(block):
    rows = block.shape[1]
    cols = block.shape[2]
    up, down = neighbours(block[:, 0:1, :], block[:, rows - 1 : rows, :], "lat")
    left, right = neighbours(block[:, :, 0], block[:, :, cols - 1], "lon")
    north = jnp.concatenate([up, lax.slice_in_dim(block, 0, rows - 1, axis=1)], 1)
    south = jnp.concatenate([lax.slice_in_dim(block, 1, rows, axis=1), down], 1)
    west = jnp.concatenate([left[:, :, None], lax.slice_in_dim(block, 0, cols - 1, axis=2)], 2)
    east = jnp.concatenate([lax.slice_in_dim(block, 1, cols, axis=2), right[:, :, None]], 2)
    return north + south + west + east - 4.0 * block


def columns(matrices, field, transpose):
    levels, height, breadth = field.shape
    blocks = matrices.shape[1]
    grouped = field.reshape(levels, height, blocks, breadth // blocks)
    form = "rbji,jrbc->irbc" if transpose else "rbij,jrbc->irbc"
    out = jnp.einsum(form, matrices, grouped, precision=lax.Precision.HIGHEST)
    return out.reshape(out.shape[0], height, breadth)


def window_gain(anchor_ref, gain_ref, s, tile_cols, tile_rows, sub, pad):
    span = FW + FH
    o = jnp.maximum(anchor_ref[s // 2, s % 2], 0)
    r = jnp.minimum(lax.div(o, tile_cols), tile_rows - FH)
    c = jnp.minimum(lax.rem(o, tile_cols), tile_cols - FW)
    c8 = pl.multiple_of(jnp.minimum(lax.div(c, FH) * FH, tile_cols - span), FH)
    off = c - c8
    g = jnp.concatenate([gain_ref[s], pad], axis=1)
    g = pltpu.roll(g, r * LTOP, 1)
    a = pltpu.roll(g[0:FH], lax.rem(off, FH), 0)
    b = pltpu.roll(g[FH:FW], lax.rem(off, FH), 0)
    low = sub >= off
    return c8, (jnp.where(low, a, 0.0), jnp.where(low, b, a), jnp.where(low, 0.0, b))


def predict_kernel(anchor_ref, top_ref, gain_ref, part_ref):
    tile_cols, wide = top_ref.shape
    slots, _, narrow = gain_ref.shape
    tile_rows = wide // LTOP
    span = FW + FH
    sub = lax.broadcasted_iota(jnp.int32, (FH, wide), 0)
    pad = jnp.zeros((FW, wide - narrow), jnp.float32)

    def predict(s, carry):
        c8, parts = window_gain(anchor_ref, gain_ref, s, tile_cols, tile_rows, sub, pad)
        win = top_ref[pl.ds(c8, span), :]
        part_ref[s] = parts[0] * win[0:FH] + parts[1] * win[FH:FW] + parts[2] * win[FW:span]
        return carry

    lax.fori_loop(0, slots, predict, 0, unroll=32)


def scatter_kernel(anchor_ref, res_ref, gain_ref, bar_ref):
    tile_cols, wide = bar_ref.shape
    slots, _, narrow = gain_ref.shape
    tile_rows = wide // LTOP
    span = FW + FH
    sub = lax.broadcasted_iota(jnp.int32, (FH, wide), 0)
    pad = jnp.zeros((FW, wide - narrow), jnp.float32)
    bar_ref[...] = jnp.zeros(bar_ref.shape, bar_ref.dtype)

    def scatter(s, carry):
        c8, parts = window_gain(anchor_ref, gain_ref, s, tile_cols, tile_rows, sub, pad)
        bar_ref[pl.ds(c8, span), :] += res_ref[s] * jnp.concatenate(parts, axis=0)
        return carry

    lax.fori_loop(0, slots, scatter, 0, unroll=16)


def predict(anchor, top, gain):
    slots = gain.shape[0]
    smem = pl.BlockSpec(memory_space=pltpu.SMEM)
    vmem = pl.BlockSpec(memory_space=pltpu.VMEM)
    return pl.pallas_call(
        predict_kernel,
        out_shape=jax.ShapeDtypeStruct((slots, FH, top.shape[1]), jnp.float32),
        in_specs=[smem, vmem, vmem],
        out_specs=vmem,
    )(anchor, top, gain)


def scatter(anchor, res, gain, top_shape):
    smem = pl.BlockSpec(memory_space=pltpu.SMEM)
    vmem = pl.BlockSpec(memory_space=pltpu.VMEM)
    return pl.pallas_call(
        scatter_kernel,
        out_shape=jax.ShapeDtypeStruct(top_shape, jnp.float32),
        in_specs=[smem, smem, vmem],
        out_specs=vmem,
    )(anchor, res, gain)


def reorder_matrix():
    source = np.arange(K)
    layer_of = source // (FH * FW)
    row_of = (source // FW) % FH
    col_of = source % FW
    matrix = np.zeros((K, K), np.float32)
    matrix[source, (col_of * FH + row_of) * LTOP + layer_of] = 1.0
    return matrix


def per_device(
    moisture,
    conductance,
    inverse,
    crop_mask,
    adjoint_in,
    foot_anchor,
    antenna_gain,
    obs_value,
    obs_weight,
):
    levels, tile_rows, tile_cols = moisture.shape
    mask_float = crop_mask.astype(jnp.float32)
    blocks = inverse.shape[1]
    matrices = inverse.reshape(tile_rows, blocks, levels, levels)

    owner_gain = antenna_gain[0, 0]
    owners, slots_per, _ = owner_gain.shape
    packed = jnp.concatenate(
        [owner_gain.reshape(owners, slots_per * K), obs_value[0, 0], obs_weight[0, 0]], -1
    )
    received = lax.all_to_all(packed, "lon", split_axis=0, concat_axis=0, tiled=True)
    slots = owners * slots_per
    gain = jnp.dot(
        received[:, : slots_per * K].reshape(slots, K), jnp.asarray(reorder_matrix()), precision=lax.Precision.HIGHEST
    )
    gain = gain.reshape(slots, FW, FH * LTOP)
    value = received[:, slots_per * K : slots_per * (K + 1)]
    weight = received[:, slots_per * (K + 1) :]

    deep = moisture[levels - LG :]
    mixed = jnp.concatenate(
        [moisture[: levels - LG], deep + conductance * stencil(deep)], 0
    )
    solved_top = columns(matrices[:, :, :LTOP, :], mixed, False)
    topmost = (solved_top * mask_float).transpose(2, 1, 0).reshape(tile_cols, tile_rows * LTOP)

    slot_anchor = foot_anchor[0, 0]
    parts = predict(slot_anchor, topmost, gain)
    predicted = jnp.sum(parts, axis=(1, 2)).reshape(owners, slots_per)
    live = (slot_anchor >= 0).astype(jnp.float32)
    residual = live * weight * (predicted - value)
    residual_out = lax.all_to_all(residual, "lon", split_axis=0, concat_axis=0, tiled=True)
    bar = scatter(slot_anchor, residual.reshape(slots), gain, topmost.shape)
    bar, residual_out = lax.optimization_barrier((bar, residual_out))

    base = columns(matrices, adjoint_in, True)
    topbar = bar.reshape(tile_cols, tile_rows, LTOP).transpose(2, 1, 0) * mask_float
    mixedbar = base + columns(matrices[:, :, :LTOP, :], topbar, True)
    deepbar = mixedbar[levels - LG :]
    gradient = jnp.concatenate(
        [mixedbar[: levels - LG], deepbar + stencil(conductance * deepbar)], 0
    )
    return gradient, residual_out[None, None]


def solution(mesh):
    in_specs = (
        P(None, "lat", "lon"),
        P("lat", "lon"),
        P("lat", "lon", None),
        P("lat", "lon"),
        P(None, "lat", "lon"),
        P("lat", "lon", None, None),
        P("lat", "lon", None, None, None),
        P("lat", "lon", None, None),
        P("lat", "lon", None, None),
    )
    out_specs = (P(None, "lat", "lon"), P("lat", "lon", None, None))
    return jax.shard_map(
        per_device, mesh=mesh, in_specs=in_specs, out_specs=out_specs, check_vma=False
    )
```

```python
import jax
import numpy as np
import jax.numpy as jnp
from jax import lax
from jax.experimental import pallas as pl
from jax.experimental.pallas import tpu as pltpu
from jax.sharding import PartitionSpec as P

LG = 8
LTOP = 4
FH = 8
FW = 16
K = 512
LANES = 128


def neighbours(edge_low, edge_high, axis):
    count = lax.axis_size(axis)
    forward = [(i, i + 1) for i in range(count - 1)]
    backward = [(target, source) for source, target in forward]
    return lax.ppermute(edge_high, axis, forward), lax.ppermute(edge_low, axis, backward)


def stencil(block):
    rows = block.shape[1]
    cols = block.shape[2]
    up, down = neighbours(block[:, 0:1, :], block[:, rows - 1 : rows, :], "lat")
    left, right = neighbours(block[:, :, 0], block[:, :, cols - 1], "lon")
    north = jnp.concatenate([up, lax.slice_in_dim(block, 0, rows - 1, axis=1)], 1)
    south = jnp.concatenate([lax.slice_in_dim(block, 1, rows, axis=1), down], 1)
    west = jnp.concatenate([left[:, :, None], lax.slice_in_dim(block, 0, cols - 1, axis=2)], 2)
    east = jnp.concatenate([lax.slice_in_dim(block, 1, cols, axis=2), right[:, :, None]], 2)
    return north + south + west + east - 4.0 * block


def columns(matrices, field, transpose):
    levels, height, breadth = field.shape
    blocks = matrices.shape[1]
    grouped = field.reshape(levels, height, blocks, breadth // blocks)
    form = "rbji,jrbc->irbc" if transpose else "rbij,jrbc->irbc"
    out = jnp.einsum(form, matrices, grouped, precision=lax.Precision.HIGHEST)
    return out.reshape(out.shape[0], height, breadth)


def window_gain(anchor_ref, gain_ref, s, tile_cols, tile_rows, sub, pad):
    span = FW + FH
    o = jnp.maximum(anchor_ref[s // 2, s % 2], 0)
    r = jnp.minimum(lax.div(o, tile_cols), tile_rows - FH)
    c = jnp.minimum(lax.rem(o, tile_cols), tile_cols - FW)
    c8 = pl.multiple_of(jnp.minimum(lax.div(c, FH) * FH, tile_cols - span), FH)
    off = c - c8
    g = jnp.concatenate([gain_ref[s], pad], axis=1)
    g = pltpu.roll(g, r * LTOP, 1)
    a = pltpu.roll(g[0:FH], lax.rem(off, FH), 0)
    b = pltpu.roll(g[FH:FW], lax.rem(off, FH), 0)
    low = sub >= off
    return c8, (jnp.where(low, a, 0.0), jnp.where(low, b, a), jnp.where(low, 0.0, b))


def predict_kernel(anchor_ref, top_ref, gain_ref, part_ref):
    tile_cols, wide = top_ref.shape
    slots, _, narrow = gain_ref.shape
    tile_rows = wide // LTOP
    span = FW + FH
    sub = lax.broadcasted_iota(jnp.int32, (FH, wide), 0)
    pad = jnp.zeros((FW, wide - narrow), jnp.float32)

    def predict(s, carry):
        c8, parts = window_gain(anchor_ref, gain_ref, s, tile_cols, tile_rows, sub, pad)
        win = top_ref[pl.ds(c8, span), :]
        acc = parts[0] * win[0:FH] + parts[1] * win[FH:FW] + parts[2] * win[FW:span]
        part_ref[s] = jnp.sum(acc, axis=0, keepdims=True)
        return carry

    lax.fori_loop(0, slots, predict, 0, unroll=16)


def scatter_kernel(anchor_ref, res_ref, gain_ref, bar_ref):
    tile_cols, wide = bar_ref.shape
    slots, _, narrow = gain_ref.shape
    tile_rows = wide // LTOP
    span = FW + FH
    sub = lax.broadcasted_iota(jnp.int32, (FH, wide), 0)
    pad = jnp.zeros((FW, wide - narrow), jnp.float32)
    bar_ref[...] = jnp.zeros(bar_ref.shape, bar_ref.dtype)

    def scatter(s, carry):
        c8, parts = window_gain(anchor_ref, gain_ref, s, tile_cols, tile_rows, sub, pad)
        bar_ref[pl.ds(c8, span), :] += res_ref[s] * jnp.concatenate(parts, axis=0)
        return carry

    lax.fori_loop(0, slots, scatter, 0, unroll=16)


def predict(anchor, top, gain):
    slots = gain.shape[0]
    smem = pl.BlockSpec(memory_space=pltpu.SMEM)
    vmem = pl.BlockSpec(memory_space=pltpu.VMEM)
    return pl.pallas_call(
        predict_kernel,
        out_shape=jax.ShapeDtypeStruct((slots, 1, top.shape[1]), jnp.float32),
        in_specs=[smem, vmem, vmem],
        out_specs=vmem,
    )(anchor, top, gain)


def scatter(anchor, res, gain, top_shape):
    smem = pl.BlockSpec(memory_space=pltpu.SMEM)
    vmem = pl.BlockSpec(memory_space=pltpu.VMEM)
    return pl.pallas_call(
        scatter_kernel,
        out_shape=jax.ShapeDtypeStruct(top_shape, jnp.float32),
        in_specs=[smem, smem, vmem],
        out_specs=vmem,
    )(anchor, res, gain)


def reorder_matrix():
    source = np.arange(K)
    layer_of = source // (FH * FW)
    row_of = (source // FW) % FH
    col_of = source % FW
    matrix = np.zeros((K, K), np.float32)
    matrix[source, (col_of * FH + row_of) * LTOP + layer_of] = 1.0
    return matrix


def per_device(
    moisture,
    conductance,
    inverse,
    crop_mask,
    adjoint_in,
    foot_anchor,
    antenna_gain,
    obs_value,
    obs_weight,
):
    levels, tile_rows, tile_cols = moisture.shape
    mask_float = crop_mask.astype(jnp.float32)
    blocks = inverse.shape[1]
    matrices = inverse.reshape(tile_rows, blocks, levels, levels)

    owner_gain = antenna_gain[0, 0]
    owners, slots_per, _ = owner_gain.shape
    packed = jnp.concatenate(
        [owner_gain.reshape(owners, slots_per * K), obs_value[0, 0], obs_weight[0, 0]], -1
    )
    received = lax.all_to_all(packed, "lon", split_axis=0, concat_axis=0, tiled=True)
    slots = owners * slots_per
    gain = jnp.dot(
        received[:, : slots_per * K].reshape(slots, K), jnp.asarray(reorder_matrix()), precision=lax.Precision.HIGHEST
    )
    gain = gain.reshape(slots, FW, FH * LTOP)
    value = received[:, slots_per * K : slots_per * (K + 1)]
    weight = received[:, slots_per * (K + 1) :]

    deep = moisture[levels - LG :]
    mixed = jnp.concatenate(
        [moisture[: levels - LG], deep + conductance * stencil(deep)], 0
    )
    solved_top = columns(matrices[:, :, :LTOP, :], mixed, False)
    topmost = (solved_top * mask_float).transpose(2, 1, 0).reshape(tile_cols, tile_rows * LTOP)

    slot_anchor = foot_anchor[0, 0]
    parts = predict(slot_anchor, topmost, gain)
    predicted = jnp.sum(parts, axis=(1, 2)).reshape(owners, slots_per)
    live = (slot_anchor >= 0).astype(jnp.float32)
    residual = live * weight * (predicted - value)
    residual_out = lax.all_to_all(residual, "lon", split_axis=0, concat_axis=0, tiled=True)
    bar = scatter(slot_anchor, residual.reshape(slots), gain, topmost.shape)
    bar, residual_out = lax.optimization_barrier((bar, residual_out))

    base = columns(matrices, adjoint_in, True)
    topbar = bar.reshape(tile_cols, tile_rows, LTOP).transpose(2, 1, 0) * mask_float
    mixedbar = base + columns(matrices[:, :, :LTOP, :], topbar, True)
    deepbar = mixedbar[levels - LG :]
    gradient = jnp.concatenate(
        [mixedbar[: levels - LG], deepbar + stencil(conductance * deepbar)], 0
    )
    return gradient, residual_out[None, None]


def solution(mesh):
    in_specs = (
        P(None, "lat", "lon"),
        P("lat", "lon"),
        P("lat", "lon", None),
        P("lat", "lon"),
        P(None, "lat", "lon"),
        P("lat", "lon", None, None),
        P("lat", "lon", None, None, None),
        P("lat", "lon", None, None),
        P("lat", "lon", None, None),
    )
    out_specs = (P(None, "lat", "lon"), P("lat", "lon", None, None))
    return jax.shard_map(
        per_device, mesh=mesh, in_specs=in_specs, out_specs=out_specs, check_vma=False
    )
```

```python
import jax
import numpy as np
import jax.numpy as jnp
from jax import lax
from jax.experimental import pallas as pl
from jax.experimental.pallas import tpu as pltpu
from jax.sharding import PartitionSpec as P

LG = 8
LTOP = 4
FH = 8
FW = 16
K = 512
LANES = 128


def neighbours(edge_low, edge_high, axis):
    count = lax.axis_size(axis)
    forward = [(i, i + 1) for i in range(count - 1)]
    backward = [(target, source) for source, target in forward]
    return lax.ppermute(edge_high, axis, forward), lax.ppermute(edge_low, axis, backward)


def stencil(block):
    rows = block.shape[1]
    cols = block.shape[2]
    up, down = neighbours(block[:, 0:1, :], block[:, rows - 1 : rows, :], "lat")
    left, right = neighbours(block[:, :, 0], block[:, :, cols - 1], "lon")
    north = jnp.concatenate([up, lax.slice_in_dim(block, 0, rows - 1, axis=1)], 1)
    south = jnp.concatenate([lax.slice_in_dim(block, 1, rows, axis=1), down], 1)
    west = jnp.concatenate([left[:, :, None], lax.slice_in_dim(block, 0, cols - 1, axis=2)], 2)
    east = jnp.concatenate([lax.slice_in_dim(block, 1, cols, axis=2), right[:, :, None]], 2)
    return north + south + west + east - 4.0 * block


def columns(matrices, field, transpose):
    levels, height, breadth = field.shape
    blocks = matrices.shape[1]
    grouped = field.reshape(levels, height, blocks, breadth // blocks)
    form = "rbji,jrbc->irbc" if transpose else "rbij,jrbc->irbc"
    out = jnp.einsum(form, matrices, grouped, precision=lax.Precision.HIGHEST)
    return out.reshape(out.shape[0], height, breadth)


def window_gain(anchor_ref, gain_ref, s, tile_cols, tile_rows, sub, pad):
    span = FW + FH
    o = jnp.maximum(anchor_ref[s // 2, s % 2], 0)
    r = jnp.minimum(lax.div(o, tile_cols), tile_rows - FH)
    c = jnp.minimum(lax.rem(o, tile_cols), tile_cols - FW)
    c8 = pl.multiple_of(jnp.minimum(lax.div(c, FH) * FH, tile_cols - span), FH)
    off = c - c8
    g = jnp.concatenate([gain_ref[s], pad], axis=1)
    g = pltpu.roll(g, r * LTOP, 1)
    a = pltpu.roll(g[0:FH], lax.rem(off, FH), 0)
    b = pltpu.roll(g[FH:FW], lax.rem(off, FH), 0)
    low = sub >= off
    return c8, (jnp.where(low, a, 0.0), jnp.where(low, b, a), jnp.where(low, 0.0, b))


def predict_kernel(anchor_ref, top_ref, gain_ref, part_ref):
    tile_cols, wide = top_ref.shape
    slots, _, narrow = gain_ref.shape
    tile_rows = wide // LTOP
    span = FW + FH
    sub = lax.broadcasted_iota(jnp.int32, (FH, wide), 0)
    pad = jnp.zeros((FW, wide - narrow), jnp.float32)

    def predict(s, carry):
        c8, parts = window_gain(anchor_ref, gain_ref, s, tile_cols, tile_rows, sub, pad)
        win = top_ref[pl.ds(c8, span), :]
        acc = parts[0] * win[0:FH] + parts[1] * win[FH:FW] + parts[2] * win[FW:span]
        part_ref[s] = jnp.sum(acc, axis=0, keepdims=True)
        return carry

    lax.fori_loop(0, slots, predict, 0, unroll=16)


def scatter_kernel(anchor_ref, res_ref, gain_ref, bar_ref):
    tile_cols, wide = bar_ref.shape
    slots, _, narrow = gain_ref.shape
    tile_rows = wide // LTOP
    span = FW + FH
    sub = lax.broadcasted_iota(jnp.int32, (FH, wide), 0)
    pad = jnp.zeros((FW, wide - narrow), jnp.float32)
    bar_ref[...] = jnp.zeros(bar_ref.shape, bar_ref.dtype)

    def scatter(s, carry):
        c8, parts = window_gain(anchor_ref, gain_ref, s, tile_cols, tile_rows, sub, pad)
        bar_ref[pl.ds(c8, span), :] += res_ref[s] * jnp.concatenate(parts, axis=0)
        return carry

    lax.fori_loop(0, slots, scatter, 0, unroll=16)


def predict(anchor, top, gain):
    slots = gain.shape[0]
    smem = pl.BlockSpec(memory_space=pltpu.SMEM)
    vmem = pl.BlockSpec(memory_space=pltpu.VMEM)
    return pl.pallas_call(
        predict_kernel,
        out_shape=jax.ShapeDtypeStruct((slots, 1, top.shape[1]), jnp.float32),
        in_specs=[smem, vmem, vmem],
        out_specs=vmem,
    )(anchor, top, gain)


def scatter(anchor, res, gain, top_shape):
    smem = pl.BlockSpec(memory_space=pltpu.SMEM)
    vmem = pl.BlockSpec(memory_space=pltpu.VMEM)
    return pl.pallas_call(
        scatter_kernel,
        out_shape=jax.ShapeDtypeStruct(top_shape, jnp.float32),
        in_specs=[smem, smem, vmem],
        out_specs=vmem,
    )(anchor, res, gain)


def reorder_matrix():
    source = np.arange(K)
    layer_of = source // (FH * FW)
    row_of = (source // FW) % FH
    col_of = source % FW
    matrix = np.zeros((K, K), np.float32)
    matrix[source, (col_of * FH + row_of) * LTOP + layer_of] = 1.0
    return matrix


def per_device(
    moisture,
    conductance,
    inverse,
    crop_mask,
    adjoint_in,
    foot_anchor,
    antenna_gain,
    obs_value,
    obs_weight,
):
    levels, tile_rows, tile_cols = moisture.shape
    mask_float = crop_mask.astype(jnp.float32)
    blocks = inverse.shape[1]
    matrices = inverse.reshape(tile_rows, blocks, levels, levels)

    owner_gain = antenna_gain[0, 0]
    owners, slots_per, _ = owner_gain.shape
    packed = jnp.concatenate(
        [owner_gain.reshape(owners, slots_per * K), obs_value[0, 0], obs_weight[0, 0]], -1
    )
    received = lax.all_to_all(packed, "lon", split_axis=0, concat_axis=0, tiled=True)
    slots = owners * slots_per
    gain = jnp.dot(
        received[:, : slots_per * K].reshape(slots, K), jnp.asarray(reorder_matrix()), precision=lax.Precision.HIGHEST
    )
    gain = gain.reshape(slots, FW, FH * LTOP)
    value = received[:, slots_per * K : slots_per * (K + 1)]
    weight = received[:, slots_per * (K + 1) :]

    deep = moisture[levels - LG :]
    mixed = jnp.concatenate(
        [moisture[: levels - LG], deep + conductance * stencil(deep)], 0
    )
    solved_top = columns(matrices[:, :, :LTOP, :], mixed, False)
    topmost = (solved_top * mask_float).transpose(2, 1, 0).reshape(tile_cols, tile_rows * LTOP)

    slot_anchor = foot_anchor[0, 0]
    parts = predict(slot_anchor, topmost, gain)
    predicted = jnp.sum(parts, axis=(1, 2)).reshape(owners, slots_per)
    live = (slot_anchor >= 0).astype(jnp.float32)
    residual = live * weight * (predicted - value)
    residual_out = lax.all_to_all(residual, "lon", split_axis=0, concat_axis=0, tiled=True)
    bar = scatter(slot_anchor, residual.reshape(slots), gain, topmost.shape)
    bar, residual_out = lax.optimization_barrier((bar, residual_out))

    base = columns(matrices, adjoint_in, True)
    topbar = bar.reshape(blocks, tile_cols // blocks, tile_rows, LTOP) * mask_float.T.reshape(
        blocks, tile_cols // blocks, tile_rows, 1
    )
    correction = jnp.einsum(
        "rbji,bcrj->irbc", matrices[:, :, :LTOP, :], topbar, precision=lax.Precision.HIGHEST
    ).reshape(levels, tile_rows, tile_cols)
    mixedbar = base + correction
    deepbar = mixedbar[levels - LG :]
    gradient = jnp.concatenate(
        [mixedbar[: levels - LG], deepbar + stencil(conductance * deepbar)], 0
    )
    return gradient, residual_out[None, None]


def solution(mesh):
    in_specs = (
        P(None, "lat", "lon"),
        P("lat", "lon"),
        P("lat", "lon", None),
        P("lat", "lon"),
        P(None, "lat", "lon"),
        P("lat", "lon", None, None),
        P("lat", "lon", None, None, None),
        P("lat", "lon", None, None),
        P("lat", "lon", None, None),
    )
    out_specs = (P(None, "lat", "lon"), P("lat", "lon", None, None))
    return jax.shard_map(
        per_device, mesh=mesh, in_specs=in_specs, out_specs=out_specs, check_vma=False
    )
```
